256 devices in a mesh: wide: 32 (over z, x), narrow: 8 (over y, core).
Axes of the slice: x: 4, y: 4, z: 8, core: 2. Of those that a mesh axis runs over, the one named last changes fastest.
Arguments:
- hidden_in: bfloat16 [64, 8192], P(None, 'wide'), may hold values from -6 to 6
- attn_gain: bfloat16 [8192], P('wide'), may hold values from 0.099609375 to 1.8984375
- qkv_weight: bfloat16 [8192, 8, 10, 128], P('wide', 'narrow'), may hold values from -2 to 2
- qkv_bias: bfloat16 [8, 10, 128], P('narrow'), may hold values from -3 to 3
- cache_keys: bfloat16 [64, 8, 4096, 128], P('wide', 'narrow'), may hold values from -256 to 256
- cache_values: bfloat16 [64, 8, 4096, 128], P('wide', 'narrow'), may hold values from -10 to 10
- positions: int32 [64, 3, 4096], P('wide'), may hold values from 0 to 4095
- lengths: int32 [64], P('wide'), may hold values from 512 to 4095, as said below
- out_weight: bfloat16 [8192, 8192], P('narrow', 'wide'), may hold values from -0.0625 to 0.0625
- mlp_gain: bfloat16 [8192], P('wide'), may hold values from 0.099609375 to 1.8984375
- gate_up_weight: bfloat16 [8192, 2, 29568], P('wide', None, 'narrow'), may hold values from -0.0625 to 0.0625
- down_weight: bfloat16 [29568, 8192], P('narrow', 'wide'), may hold values from -0.03125 to 0.03125
Outputs:
- layer_out: bfloat16 [64, 8192], P(None, 'wide')
The draws below stay inside these ranges and needn't reach their ends.
Inputs may be any that keep to these rules, and one draw needn't show every extreme that they name: Slots 0 to lengths[b] - 1 of request b are filled, the new token takes slot lengths[b], and some request has 4095.
All inputs are finite; a program needn't handle non-finite values.
Results may differ from the reference program's by a relative error of at most 0.01115.
The reference program's roundings to bfloat16 on the way count: a program that leaves them out, or rounds other values in their place, can miss the bound.
Values may be sent and summed in bfloat16 or wider, within the bound.
No kernel may reach another device: no remote copies, remote signals or barrier semaphores. Data moves between devices by JAX's collectives and lax.ppermute only.
A program may use at most 64 MiB of HBM per device.

```python
import math
import jax
import jax.numpy as jnp
from jax import lax

D = 8192
H = 64
KVH = 8
DH = 128
FF = 29568
GROUP = 8
REQS = 64
CACHE = 4096


def draw_qkv_weight(key, part):
    shape = (D, KVH, GROUP + 2, DH)
    key_noise, key_mix = jax.random.split(key)
    noise = jnp.clip(jax.random.normal(key_noise, shape, jnp.float32), -6.0, 6.0)
    affinity = jax.random.uniform(key_mix, (1, KVH, GROUP + 2, 1), jnp.float32, 0.0, 0.4)
    slot_index = jnp.arange(GROUP + 2)[None, None, :, None]
    affinity = jnp.where(slot_index < GROUP, affinity, 0.0)
    key_part = noise[:, :, GROUP:GROUP + 1, :]
    mixed = jnp.sqrt(1.0 - affinity * affinity) * noise + affinity * key_part
    return (mixed * math.sqrt(2.5 / D)).astype(jnp.bfloat16)


def draw_cache_keys(key, part):
    shape = (REQS, KVH, CACHE, DH)
    return (jnp.clip(jax.random.normal(key, shape, jnp.float32), -6.25, 6.25) * 1.6).astype(jnp.bfloat16)


def draw_lengths(key, part):
    key_length, key_longest = jax.random.split(key)
    values = jax.random.randint(key_length, (REQS,), CACHE // 8, CACHE)
    longest = jax.random.randint(key_longest, (), 0, REQS)
    return jnp.where(jnp.arange(REQS) == longest, CACHE - 1, values).astype(jnp.int32)


def set_ends(values, stream_key, low, high):
    longest = values.shape.index(max(values.shape))
    spots = []
    for shift in (0, 1):
        where = [jax.random.randint(jax.random.fold_in(stream_key, axis), (), 0, length) for axis, length in enumerate(values.shape)]
        where[longest] = (where[longest] + shift) % values.shape[longest]
        spots.append(tuple(where))
    return values.at[spots[0]].set(low).at[spots[1]].set(high)


def with_spikes(entries, rng, source, target, parts, factor):
    def block_of(dim):
        return (jnp.arange(entries.shape[dim]) // (entries.shape[dim] // parts)).reshape((-1,) + (1,) * (entries.ndim - 1 - dim))

    first = jax.random.permutation(rng, parts)[block_of(target)]
    other_side = (block_of(target) + parts // 2) % parts
    return jnp.where((block_of(source) == first) | (block_of(source) == other_side), factor * entries, entries)


def level_of(own_key, dims, cuts, least, top_value):
    def one(dim, parts):
        draws = jax.random.uniform(jax.random.fold_in(jax.random.fold_in(own_key, 6), dim), (parts,), jnp.float32, least / len(cuts), top_value / len(cuts))
        return jnp.repeat(jnp.exp(draws), dims[dim] // parts).reshape((-1,) + (1,) * (len(dims) - dim - 1))

    level = one(*cuts[0])
    for cut in cuts[1:]:
        level = level * one(*cut)
    return level


def gaussian(stream_key, dims, scale, most, shards=(), kind=jnp.bfloat16):
    values = scale * jax.random.normal(stream_key, dims, jnp.float32)
    if shards:
        values = values * level_of(stream_key, dims, shards, -0.22, 0.18)
    return jnp.clip(values, -most, most).astype(kind)


def bell_draw_with(rng, shape, scale, most, shards, heavy, held_as=jnp.bfloat16):
    array = scale * jax.random.normal(rng, shape, jnp.float32)
    if shards:
        array = array * level_of(rng, shape, shards, -0.22, 0.18)
    return jnp.clip(with_spikes(array, jax.random.fold_in(rng, 3), *heavy), -most, most).astype(held_as)


def setup_inputs(seed: int = 0) -> dict:
    key_list = jax.random.split(jax.random.key(seed), 13)
    hidden_in = bell_draw_with(key_list[0], (REQS, D), 1.0, 6.0, ((1, 32),), (1, 0, 32, 2.75))
    attn_gain = jnp.clip(1.0 + 0.18 * jax.random.normal(key_list[1], (D,), jnp.float32), 0.099609375, 1.8984375).astype(jnp.bfloat16)
    qkv_weight = draw_qkv_weight(jax.random.fold_in(key_list[12], 71), 0)
    qkv_bias = gaussian(key_list[3], (KVH, GROUP + 2, DH), 0.5, 3.0, ((0, 8),))
    cache_keys = draw_cache_keys(jax.random.fold_in(key_list[12], 71), 0)
    cache_values = gaussian(key_list[5], (REQS, KVH, CACHE, DH), 1.6, 10.0, ((0, 32), (1, 8)))
    positions = set_ends(jax.random.randint(key_list[6], (REQS, 3, CACHE), 0, CACHE), jax.random.fold_in(key_list[6], 1), 0, CACHE - 1).astype(jnp.int32)
    lengths = draw_lengths(jax.random.fold_in(key_list[12], 71), 0)
    out_weight = gaussian(key_list[8], (H * DH, D), (H * DH) ** -0.5, 0.0625, ((0, 8), (1, 32)))
    mlp_gain = jnp.clip(1.0 + 0.18 * jax.random.normal(key_list[9], (D,), jnp.float32), 0.099609375, 1.8984375).astype(jnp.bfloat16)
    gate_up_weight = gaussian(key_list[10], (D, 2, FF), D ** -0.5, 0.0625, ((0, 32), (2, 8)))
    down_weight = gaussian(key_list[11], (FF, D), FF ** -0.5, 0.03125, ((0, 8), (1, 32)))
    return dict(hidden_in=hidden_in, attn_gain=attn_gain, qkv_weight=qkv_weight, qkv_bias=qkv_bias, cache_keys=cache_keys, cache_values=cache_values, positions=positions, lengths=lengths, out_weight=out_weight, mlp_gain=mlp_gain, gate_up_weight=gate_up_weight, down_weight=down_weight)


norm_eps = 1e-06
rope_base = 1000000.0

def mrope_tables(position):
    half_width = DH // 2
    pair_index = jnp.arange(half_width)
    inv_freq = jnp.exp(pair_index.astype(jnp.float32) * (-2.0 * math.log(rope_base) / DH))
    component = (pair_index >= DH // 8).astype(jnp.int32) + (pair_index >= DH // 8 + 3 * DH // 16).astype(jnp.int32)
    pos_float = position.astype(jnp.float32)
    chosen = jnp.where(component == 0, pos_float[..., 0, :, None], jnp.where(component == 1, pos_float[..., 1, :, None], pos_float[..., 2, :, None]))
    angles = chosen * inv_freq
    return (jnp.cos(angles), jnp.sin(angles))

def rotate(values, cosine, sine_table):
    half_width = values.shape[-1] // 2
    leading = values[..., :half_width]
    trailing = values[..., half_width:]
    return jnp.concatenate([leading * cosine - trailing * sine_table, trailing * cosine + leading * sine_table], axis=-1)

def reference(hidden_in, attn_gain, qkv_weight, qkv_bias, cache_keys, cache_values, positions, lengths, out_weight, mlp_gain, gate_up_weight, down_weight):
    score_scale = 1.0 / math.sqrt(DH)
    inputs = hidden_in.astype(jnp.float32)
    inv_rms = 1.0 / jnp.sqrt(lax.optimization_barrier(jnp.sum(inputs * inputs, axis=1)) / D + norm_eps)
    scaled = (inputs * attn_gain.astype(jnp.float32)).astype(jnp.bfloat16)
    width = KVH * (GROUP + 2) * DH
    projected = jnp.dot(scaled, qkv_weight.reshape(D, width), preferred_element_type=jnp.float32)
    projected = inv_rms[:, None] * projected + qkv_bias.reshape(width).astype(jnp.float32)
    projected = projected.reshape(REQS, KVH, GROUP + 2, DH)
    new_position = jnp.take_along_axis(positions, lengths.astype(jnp.int32)[:, None, None], axis=2)
    cos_new, sin_new = mrope_tables(new_position)
    query = rotate(projected[:, :, :GROUP], cos_new[:, None], sin_new[:, None]).astype(jnp.bfloat16)
    key_new = rotate(projected[:, :, GROUP], cos_new, sin_new).astype(jnp.bfloat16)
    value_new = projected[:, :, GROUP + 1].astype(jnp.bfloat16)

    def one_request(items):
        req_query, req_key, req_value, req_keys, req_values, req_pos, req_length = items
        cosine, sine_table = mrope_tables(req_pos)
        keys_rot = rotate(req_keys.astype(jnp.float32), cosine[None], sine_table[None]).astype(jnp.bfloat16)
        scores = jnp.einsum('gjd,gsd->gjs', req_query.astype(jnp.float32), keys_rot.astype(jnp.float32)) * score_scale
        own_score = jnp.einsum('gjd,gd->gj', req_query.astype(jnp.float32), req_key.astype(jnp.float32)) * score_scale
        valid_slot = jnp.arange(CACHE) < req_length
        row_max = jnp.maximum(lax.optimization_barrier(jnp.max(jnp.where(valid_slot, scores, -jnp.inf), axis=2)), own_score)
        probabilities = jnp.where(valid_slot, jnp.exp(scores - row_max[..., None]), 0.0)
        own_prob = jnp.exp(own_score - row_max)
        totals = lax.optimization_barrier(jnp.sum(probabilities, axis=2)) + own_prob
        probs_rounded = lax.optimization_barrier(probabilities.astype(jnp.bfloat16)).astype(jnp.float32)
        own_rounded = lax.optimization_barrier(own_prob.astype(jnp.bfloat16)).astype(jnp.float32)
        weighted = jnp.einsum('gjs,gsd->gjd', probs_rounded, req_values.astype(jnp.float32))
        weighted = weighted + own_rounded[..., None] * req_value.astype(jnp.float32)[:, None, :]
        return (weighted / totals[..., None]).astype(jnp.bfloat16)
    attended = lax.map(one_request, (query, key_new, value_new, cache_keys, cache_values, positions, lengths))
    attended = attended.reshape(REQS, H * DH)
    attn_out = jnp.dot(attended, out_weight, preferred_element_type=jnp.float32)
    residual = (inputs + attn_out).astype(jnp.bfloat16)
    resid_float = residual.astype(jnp.float32)
    inv_rms2 = 1.0 / jnp.sqrt(lax.optimization_barrier(jnp.sum(resid_float * resid_float, axis=1)) / D + norm_eps)
    scaled2 = (resid_float * mlp_gain.astype(jnp.float32)).astype(jnp.bfloat16)
    gate_up = jnp.dot(scaled2, gate_up_weight.reshape(D, 2 * FF), preferred_element_type=jnp.float32) * inv_rms2[:, None]
    hidden = (jax.nn.silu(gate_up[:, :FF]) * gate_up[:, FF:]).astype(jnp.bfloat16)
    mlp_out = jnp.dot(hidden, down_weight, preferred_element_type=jnp.float32)
    return (resid_float + mlp_out).astype(jnp.bfloat16)
```

```python
import math

import jax
import jax.numpy as jnp
from jax import lax
from jax.sharding import PartitionSpec as P

D = 8192
DH = 128
CACHE = 4096


norm_eps = 1e-06
rope_base = 1000000.0


def mrope_tables(position):
    half_width = DH // 2
    pair_index = jnp.arange(half_width)
    inv_freq = jnp.exp(pair_index.astype(jnp.float32) * (-2.0 * math.log(rope_base) / DH))
    component = (pair_index >= DH // 8).astype(jnp.int32) + (
        pair_index >= DH // 8 + 3 * DH // 16
    ).astype(jnp.int32)
    pos_float = position.astype(jnp.float32)
    chosen = jnp.where(
        component == 0,
        pos_float[..., 0, :, None],
        jnp.where(component == 1, pos_float[..., 1, :, None], pos_float[..., 2, :, None]),
    )
    angles = chosen * inv_freq
    return (jnp.cos(angles), jnp.sin(angles))


def rotate(values, cosine, sine_table):
    half_width = values.shape[-1] // 2
    leading = values[..., :half_width]
    trailing = values[..., half_width:]
    return jnp.concatenate(
        [leading * cosine - trailing * sine_table, trailing * cosine + leading * sine_table],
        axis=-1,
    )


def local(
    hidden_in,
    attn_gain,
    qkv_weight,
    qkv_bias,
    cache_keys,
    cache_values,
    positions,
    lengths,
    out_weight,
    mlp_gain,
    gate_up_weight,
    down_weight,
):
    score_scale = 1.0 / math.sqrt(DH)
    owned = lengths.shape[0]
    local_rows = hidden_in.shape[1]
    kv_local = qkv_weight.shape[1]
    slot_count = qkv_weight.shape[2]
    group_size = slot_count - 2
    width = kv_local * slot_count * DH
    inputs = hidden_in.astype(jnp.float32)
    local_squares = jnp.sum(inputs * inputs, axis=1)
    scaled = (inputs * attn_gain.astype(jnp.float32)).astype(jnp.bfloat16)
    weight_flat = qkv_weight.reshape(local_rows, width)
    partial = jnp.dot(scaled, weight_flat, preferred_element_type=jnp.float32)
    summed = lax.psum_scatter(
        jnp.concatenate([partial, local_squares[:, None]], axis=1),
        "wide",
        scatter_dimension=0,
        tiled=True,
    )
    inv_rms = 1.0 / jnp.sqrt(summed[:, width] / D + norm_eps)
    projected = inv_rms[:, None] * summed[:, :width] + qkv_bias.reshape(width).astype(jnp.float32)
    projected = projected.reshape(owned, kv_local, slot_count, DH)
    cosine, sine_table = mrope_tables(positions)
    keys_rot = rotate(cache_keys.astype(jnp.float32), cosine[:, None], sine_table[:, None]).astype(
        jnp.bfloat16
    )
    new_position = jnp.take_along_axis(positions, lengths[:, None, None], axis=2)
    cos_new, sin_new = mrope_tables(new_position)
    query = rotate(projected[:, :, :group_size], cos_new[:, None], sin_new[:, None]).astype(
        jnp.bfloat16
    )
    key_new = rotate(projected[:, :, group_size], cos_new, sin_new).astype(jnp.bfloat16)
    value_new = projected[:, :, group_size + 1].astype(jnp.bfloat16)
    scores = (
        jnp.einsum("rgjd,rgsd->rgjs", query, keys_rot, preferred_element_type=jnp.float32)
        * score_scale
    )
    own_score = (
        jnp.sum(query.astype(jnp.float32) * key_new.astype(jnp.float32)[:, :, None, :], axis=3)
        * score_scale
    )
    valid_slot = jnp.arange(CACHE)[None, None, None, :] < lengths[:, None, None, None]
    row_max = jnp.maximum(jnp.max(jnp.where(valid_slot, scores, -jnp.inf), axis=3), own_score)
    probabilities = jnp.where(valid_slot, jnp.exp(scores - row_max[..., None]), 0.0)
    own_prob = jnp.exp(own_score - row_max)
    totals = jnp.sum(probabilities, axis=3) + own_prob
    probs_rounded = probabilities.astype(jnp.bfloat16)
    own_rounded = own_prob.astype(jnp.bfloat16).astype(jnp.float32)
    weighted = jnp.einsum(
        "rgjs,rgsd->rgjd", probs_rounded, cache_values, preferred_element_type=jnp.float32
    )
    weighted = weighted + own_rounded[..., None] * value_new.astype(jnp.float32)[:, :, None, :]
    attended = (
        (weighted / totals[..., None])
        .astype(jnp.bfloat16)
        .reshape(owned, kv_local * group_size * DH)
    )
    head_partial = jnp.dot(
        lax.all_gather(attended, "wide", axis=0, tiled=True),
        out_weight,
        preferred_element_type=jnp.float32,
    )
    attn_out = lax.psum(head_partial, "narrow")
    residual = (inputs + attn_out).astype(jnp.bfloat16)
    resid_float = residual.astype(jnp.float32)
    resid_squares = jnp.sum(resid_float * resid_float, axis=1)
    scaled2 = (resid_float * mlp_gain.astype(jnp.float32)).astype(jnp.bfloat16)
    hidden_local = gate_up_weight.shape[2]
    gate_up_flat = gate_up_weight.reshape(local_rows, 2 * hidden_local)
    partial2 = jnp.dot(scaled2, gate_up_flat, preferred_element_type=jnp.float32)
    summed2 = lax.psum(jnp.concatenate([partial2, resid_squares[:, None]], axis=1), "wide")
    inv_rms2 = 1.0 / jnp.sqrt(summed2[:, 2 * hidden_local] / D + norm_eps)
    gate_up = summed2[:, : 2 * hidden_local] * inv_rms2[:, None]
    hidden = (jax.nn.silu(gate_up[:, :hidden_local]) * gate_up[:, hidden_local:]).astype(
        jnp.bfloat16
    )
    down_partial = jnp.dot(hidden, down_weight, preferred_element_type=jnp.float32)
    mlp_out = lax.psum(down_partial, "narrow")
    return (resid_float + mlp_out).astype(jnp.bfloat16)


def solution(mesh):
    in_specs = (
        P(None, "wide"),
        P("wide"),
        P("wide", "narrow", None, None),
        P("narrow", None, None),
        P("wide", "narrow", None, None),
        P("wide", "narrow", None, None),
        P("wide", None, None),
        P("wide"),
        P("narrow", "wide"),
        P("wide"),
        P("wide", None, "narrow"),
        P("narrow", "wide"),
    )
    out_specs = P(None, "wide")
    return jax.shard_map(local, mesh=mesh, in_specs=in_specs, out_specs=out_specs, check_vma=False)
```

```python
import math

import jax
import jax.numpy as jnp
from jax import lax
from jax.sharding import PartitionSpec as P

D = 8192
DH = 128
CACHE = 4096


norm_eps = 1e-06
rope_base = 1000000.0


def mrope_tables(position):
    half_width = DH // 2
    pair_index = jnp.arange(half_width)
    inv_freq = jnp.exp(pair_index.astype(jnp.float32) * (-2.0 * math.log(rope_base) / DH))
    component = (pair_index >= DH // 8).astype(jnp.int32) + (
        pair_index >= DH // 8 + 3 * DH // 16
    ).astype(jnp.int32)
    pos_float = position.astype(jnp.float32)
    chosen = jnp.where(
        component == 0,
        pos_float[..., 0, :, None],
        jnp.where(component == 1, pos_float[..., 1, :, None], pos_float[..., 2, :, None]),
    )
    angles = chosen * inv_freq
    return (jnp.cos(angles), jnp.sin(angles))


def rotate(values, cosine, sine_table):
    half_width = values.shape[-1] // 2
    leading = values[..., :half_width]
    trailing = values[..., half_width:]
    return jnp.concatenate(
        [leading * cosine - trailing * sine_table, trailing * cosine + leading * sine_table],
        axis=-1,
    )


def reduce_rows(x, axis):
    n = lax.axis_size(axis)
    blocks = x.reshape(n, x.shape[0] // n, x.shape[1])
    return jnp.sum(lax.all_to_all(blocks, axis, 0, 0, tiled=False), axis=0)


def gather_rows(x, axis):
    n = lax.axis_size(axis)
    copies = jnp.broadcast_to(x[None], (n,) + x.shape)
    return lax.all_to_all(copies, axis, 0, 0, tiled=False).reshape(n * x.shape[0], x.shape[1])


def sum_all(x, axis):
    n = lax.axis_size(axis)
    step = 1
    while step < n:
        x = x + lax.ppermute(x, axis, [(i, i ^ step) for i in range(n)])
        step *= 2
    return x


def local(
    hidden_in,
    attn_gain,
    qkv_weight,
    qkv_bias,
    cache_keys,
    cache_values,
    positions,
    lengths,
    out_weight,
    mlp_gain,
    gate_up_weight,
    down_weight,
):
    score_scale = 1.0 / math.sqrt(DH)
    owned = lengths.shape[0]
    local_rows = hidden_in.shape[1]
    kv_local = qkv_weight.shape[1]
    slot_count = qkv_weight.shape[2]
    group_size = slot_count - 2
    width = kv_local * slot_count * DH
    inputs = hidden_in.astype(jnp.float32)
    local_squares = jnp.sum(inputs * inputs, axis=1)
    scaled = (inputs * attn_gain.astype(jnp.float32)).astype(jnp.bfloat16)
    weight_flat = qkv_weight.reshape(local_rows, width)
    partial = jnp.dot(scaled, weight_flat, preferred_element_type=jnp.float32)
    summed = reduce_rows(jnp.concatenate([partial, local_squares[:, None]], axis=1), "wide")
    inv_rms = 1.0 / jnp.sqrt(summed[:, width] / D + norm_eps)
    projected = inv_rms[:, None] * summed[:, :width] + qkv_bias.reshape(width).astype(jnp.float32)
    projected = projected.reshape(owned, kv_local, slot_count, DH)
    cosine, sine_table = mrope_tables(positions)
    keys_rot = rotate(cache_keys.astype(jnp.float32), cosine[:, None], sine_table[:, None]).astype(
        jnp.bfloat16
    )
    new_position = jnp.take_along_axis(positions, lengths[:, None, None], axis=2)
    cos_new, sin_new = mrope_tables(new_position)
    query = rotate(projected[:, :, :group_size], cos_new[:, None], sin_new[:, None]).astype(
        jnp.bfloat16
    )
    key_new = rotate(projected[:, :, group_size], cos_new, sin_new).astype(jnp.bfloat16)
    value_new = projected[:, :, group_size + 1].astype(jnp.bfloat16)
    scores = (
        jnp.einsum("rgjd,rgsd->rgjs", query, keys_rot, preferred_element_type=jnp.float32)
        * score_scale
    )
    own_score = (
        jnp.sum(query.astype(jnp.float32) * key_new.astype(jnp.float32)[:, :, None, :], axis=3)
        * score_scale
    )
    valid_slot = jnp.arange(CACHE)[None, None, None, :] < lengths[:, None, None, None]
    row_max = jnp.maximum(jnp.max(jnp.where(valid_slot, scores, -jnp.inf), axis=3), own_score)
    probabilities = jnp.where(valid_slot, jnp.exp(scores - row_max[..., None]), 0.0)
    own_prob = jnp.exp(own_score - row_max)
    totals = jnp.sum(probabilities, axis=3) + own_prob
    probs_rounded = probabilities.astype(jnp.bfloat16)
    own_rounded = own_prob.astype(jnp.bfloat16).astype(jnp.float32)
    weighted = jnp.einsum(
        "rgjs,rgsd->rgjd", probs_rounded, cache_values, preferred_element_type=jnp.float32
    )
    weighted = weighted + own_rounded[..., None] * value_new.astype(jnp.float32)[:, :, None, :]
    attended = (
        (weighted / totals[..., None])
        .astype(jnp.bfloat16)
        .reshape(owned, kv_local * group_size * DH)
    )
    head_partial = jnp.dot(
        gather_rows(attended, "wide"),
        out_weight,
        preferred_element_type=jnp.float32,
    )
    attn_out = sum_all(head_partial, "narrow")
    residual = (inputs + attn_out).astype(jnp.bfloat16)
    resid_float = residual.astype(jnp.float32)
    resid_squares = jnp.sum(resid_float * resid_float, axis=1)
    scaled2 = (resid_float * mlp_gain.astype(jnp.float32)).astype(jnp.bfloat16)
    hidden_local = gate_up_weight.shape[2]
    gate_up_flat = gate_up_weight.reshape(local_rows, 2 * hidden_local)
    partial2 = jnp.dot(scaled2, gate_up_flat, preferred_element_type=jnp.float32)
    summed2 = reduce_rows(jnp.concatenate([partial2, resid_squares[:, None]], axis=1), "wide")
    inv_rms2 = 1.0 / jnp.sqrt(summed2[:, 2 * hidden_local] / D + norm_eps)
    gate_up = summed2[:, : 2 * hidden_local] * inv_rms2[:, None]
    hidden = (jax.nn.silu(gate_up[:, :hidden_local]) * gate_up[:, hidden_local:]).astype(
        jnp.bfloat16
    )
    down_partial = jnp.dot(gather_rows(hidden, "wide"), down_weight, preferred_element_type=jnp.float32)
    mlp_out = sum_all(down_partial, "narrow")
    return (resid_float + mlp_out).astype(jnp.bfloat16)


def solution(mesh):
    in_specs = (
        P(None, "wide"),
        P("wide"),
        P("wide", "narrow", None, None),
        P("narrow", None, None),
        P("wide", "narrow", None, None),
        P("wide", "narrow", None, None),
        P("wide", None, None),
        P("wide"),
        P("narrow", "wide"),
        P("wide"),
        P("wide", None, "narrow"),
        P("narrow", "wide"),
    )
    out_specs = P(None, "wide")
    return jax.shard_map(local, mesh=mesh, in_specs=in_specs, out_specs=out_specs, check_vma=False)
```

```python
import math

import jax
import jax.numpy as jnp
from jax import lax
from jax.sharding import PartitionSpec as P

D = 8192
DH = 128
CACHE = 4096


norm_eps = 1e-06
rope_base = 1000000.0


def mrope_tables(position):
    half_width = DH // 2
    pair_index = jnp.arange(half_width)
    inv_freq = jnp.exp(pair_index.astype(jnp.float32) * (-2.0 * math.log(rope_base) / DH))
    component = (pair_index >= DH // 8).astype(jnp.int32) + (
        pair_index >= DH // 8 + 3 * DH // 16
    ).astype(jnp.int32)
    pos_float = position.astype(jnp.float32)
    chosen = jnp.where(
        component == 0,
        pos_float[..., 0, :, None],
        jnp.where(component == 1, pos_float[..., 1, :, None], pos_float[..., 2, :, None]),
    )
    angles = chosen * inv_freq
    return (jnp.cos(angles), jnp.sin(angles))


def rotate(values, cosine, sine_table):
    half_width = values.shape[-1] // 2
    leading = values[..., :half_width]
    trailing = values[..., half_width:]
    return jnp.concatenate(
        [leading * cosine - trailing * sine_table, trailing * cosine + leading * sine_table],
        axis=-1,
    )


def reduce_rows(x, axis):
    n = lax.axis_size(axis)
    blocks = x.reshape(n, x.shape[0] // n, x.shape[1])
    return jnp.sum(lax.all_to_all(blocks, axis, 0, 0, tiled=False), axis=0)


def gather_rows(x, axis):
    n = lax.axis_size(axis)
    copies = jnp.broadcast_to(x[None], (n,) + x.shape)
    return lax.all_to_all(copies, axis, 0, 0, tiled=False).reshape(n * x.shape[0], x.shape[1])


def sum_all(x, axis):
    n = lax.axis_size(axis)
    step = 1
    while step < n:
        x = x + lax.ppermute(x, axis, [(i, i ^ step) for i in range(n)])
        step *= 2
    return x


def local(
    hidden_in,
    attn_gain,
    qkv_weight,
    qkv_bias,
    cache_keys,
    cache_values,
    positions,
    lengths,
    out_weight,
    mlp_gain,
    gate_up_weight,
    down_weight,
):
    score_scale = 1.0 / math.sqrt(DH)
    owned = lengths.shape[0]
    local_rows = hidden_in.shape[1]
    kv_local = qkv_weight.shape[1]
    slot_count = qkv_weight.shape[2]
    group_size = slot_count - 2
    width = kv_local * slot_count * DH
    inputs = hidden_in.astype(jnp.float32)
    local_squares = jnp.sum(inputs * inputs, axis=1)
    scaled = (inputs * attn_gain.astype(jnp.float32)).astype(jnp.bfloat16)
    weight_flat = qkv_weight.reshape(local_rows, width)
    partial = jnp.dot(scaled, weight_flat, preferred_element_type=jnp.float32)
    summed = reduce_rows(jnp.concatenate([partial, local_squares[:, None]], axis=1), "wide")
    inv_rms = 1.0 / jnp.sqrt(summed[:, width] / D + norm_eps)
    projected = inv_rms[:, None] * summed[:, :width] + qkv_bias.reshape(width).astype(jnp.float32)
    projected = projected.reshape(owned, kv_local, slot_count, DH)
    cosine, sine_table = mrope_tables(positions)
    keys_rot = rotate(cache_keys.astype(jnp.float32), cosine[:, None], sine_table[:, None]).astype(
        jnp.bfloat16
    )
    new_position = jnp.take_along_axis(positions, lengths[:, None, None], axis=2)
    cos_new, sin_new = mrope_tables(new_position)
    query = rotate(projected[:, :, :group_size], cos_new[:, None], sin_new[:, None]).astype(
        jnp.bfloat16
    )
    key_new = rotate(projected[:, :, group_size], cos_new, sin_new).astype(jnp.bfloat16)
    value_new = projected[:, :, group_size + 1].astype(jnp.bfloat16)
    scores = (
        jnp.einsum("rgjd,rgsd->rgjs", query, keys_rot, preferred_element_type=jnp.float32)
        * score_scale
    )
    own_score = (
        jnp.sum(query.astype(jnp.float32) * key_new.astype(jnp.float32)[:, :, None, :], axis=3)
        * score_scale
    )
    valid_slot = jnp.arange(CACHE)[None, None, None, :] < lengths[:, None, None, None]
    row_max = jnp.maximum(jnp.max(jnp.where(valid_slot, scores, -jnp.inf), axis=3), own_score)
    probabilities = jnp.where(valid_slot, jnp.exp(scores - row_max[..., None]), 0.0)
    own_prob = jnp.exp(own_score - row_max)
    totals = jnp.sum(probabilities, axis=3) + own_prob
    probs_rounded = probabilities.astype(jnp.bfloat16)
    own_rounded = own_prob.astype(jnp.bfloat16).astype(jnp.float32)
    weighted = jnp.einsum(
        "rgjs,rgsd->rgjd", probs_rounded, cache_values, preferred_element_type=jnp.float32
    )
    weighted = weighted + own_rounded[..., None] * value_new.astype(jnp.float32)[:, :, None, :]
    attended = (
        (weighted / totals[..., None])
        .astype(jnp.bfloat16)
        .reshape(owned, kv_local * group_size * DH)
    )
    head_partial = jnp.dot(
        gather_rows(attended, "wide"),
        out_weight,
        preferred_element_type=jnp.float32,
    )
    attn_out = sum_all(head_partial, "narrow")
    residual = (inputs + attn_out).astype(jnp.bfloat16)
    resid_float = residual.astype(jnp.float32)
    resid_squares = jnp.sum(resid_float * resid_float, axis=1)
    scaled2 = (resid_float * mlp_gain.astype(jnp.float32)).astype(jnp.bfloat16)
    hidden_local = gate_up_weight.shape[2]
    gate_up_flat = gate_up_weight.reshape(local_rows, 2 * hidden_local)
    partial2 = jnp.dot(scaled2, gate_up_flat, preferred_element_type=jnp.float32)
    squares_hi = resid_squares.astype(jnp.bfloat16)
    squares_lo = (resid_squares - squares_hi.astype(jnp.float32)).astype(jnp.bfloat16)
    sent2 = jnp.concatenate(
        [partial2.astype(jnp.bfloat16), squares_hi[:, None], squares_lo[:, None]], axis=1
    )
    n_wide = lax.axis_size("wide")
    received2 = lax.all_to_all(
        sent2.reshape(n_wide, sent2.shape[0] // n_wide, sent2.shape[1]), "wide", 0, 0, tiled=False
    )
    summed2 = jnp.sum(received2.astype(jnp.float32), axis=0)
    total_squares2 = summed2[:, 2 * hidden_local] + summed2[:, 2 * hidden_local + 1]
    inv_rms2 = 1.0 / jnp.sqrt(total_squares2 / D + norm_eps)
    gate_up = summed2[:, : 2 * hidden_local] * inv_rms2[:, None]
    hidden = (jax.nn.silu(gate_up[:, :hidden_local]) * gate_up[:, hidden_local:]).astype(
        jnp.bfloat16
    )
    down_partial = jnp.dot(gather_rows(hidden, "wide"), down_weight, preferred_element_type=jnp.float32)
    mlp_out = sum_all(down_partial, "narrow")
    return (resid_float + mlp_out).astype(jnp.bfloat16)


def solution(mesh):
    in_specs = (
        P(None, "wide"),
        P("wide"),
        P("wide", "narrow", None, None),
        P("narrow", None, None),
        P("wide", "narrow", None, None),
        P("wide", "narrow", None, None),
        P("wide", None, None),
        P("wide"),
        P("narrow", "wide"),
        P("wide"),
        P("wide", None, "narrow"),
        P("narrow", "wide"),
    )
    out_specs = P(None, "wide")
    return jax.shard_map(local, mesh=mesh, in_specs=in_specs, out_specs=out_specs, check_vma=False)
```

```python
import math

import jax
import jax.numpy as jnp
from jax import lax
from jax.sharding import PartitionSpec as P

D = 8192
DH = 128
CACHE = 4096


norm_eps = 1e-06
rope_base = 1000000.0


def cos_sin(angle):
    k = jnp.round(angle * 0.6366197723675814)
    r = ((angle - k * 1.5703125) - k * 4.837512969970703125e-4) - k * 7.54978995489188216e-8
    z = r * r
    s = r + r * z * (-1.6666654611e-1 + z * (8.3321608736e-3 + z * -1.9515295891e-4))
    c = 1.0 - 0.5 * z + z * z * (
        4.166664568298827e-2 + z * (-1.388731625493765e-3 + z * 2.443315711809948e-5)
    )
    q = k.astype(jnp.int32) % 4
    cos = jnp.where(q == 0, c, jnp.where(q == 1, -s, jnp.where(q == 2, -c, s)))
    sin = jnp.where(q == 0, s, jnp.where(q == 1, c, jnp.where(q == 2, -s, -c)))
    return cos, sin


def mrope_tables(position):
    half_width = DH // 2
    pair_index = jnp.arange(half_width)
    inv_freq = jnp.exp(pair_index.astype(jnp.float32) * (-2.0 * math.log(rope_base) / DH))
    component = (pair_index >= DH // 8).astype(jnp.int32) + (
        pair_index >= DH // 8 + 3 * DH // 16
    ).astype(jnp.int32)
    pos_float = position.astype(jnp.float32)
    chosen = jnp.where(
        component == 0,
        pos_float[..., 0, :, None],
        jnp.where(component == 1, pos_float[..., 1, :, None], pos_float[..., 2, :, None]),
    )
    angles = chosen * inv_freq
    return cos_sin(angles)


def rotate(values, cosine, sine_table):
    half_width = values.shape[-1] // 2
    leading = values[..., :half_width]
    trailing = values[..., half_width:]
    return jnp.concatenate(
        [leading * cosine - trailing * sine_table, trailing * cosine + leading * sine_table],
        axis=-1,
    )


def reduce_rows(x, axis):
    n = lax.axis_size(axis)
    blocks = x.reshape(n, x.shape[0] // n, x.shape[1])
    return jnp.sum(lax.all_to_all(blocks, axis, 0, 0, tiled=False), axis=0)


def gather_rows(x, axis):
    n = lax.axis_size(axis)
    copies = jnp.broadcast_to(x[None], (n,) + x.shape)
    return lax.all_to_all(copies, axis, 0, 0, tiled=False).reshape(n * x.shape[0], x.shape[1])


def sum_all(x, axis):
    n = lax.axis_size(axis)
    step = 1
    while step < n:
        x = x + lax.ppermute(x, axis, [(i, i ^ step) for i in range(n)])
        step *= 2
    return x


def local(
    hidden_in,
    attn_gain,
    qkv_weight,
    qkv_bias,
    cache_keys,
    cache_values,
    positions,
    lengths,
    out_weight,
    mlp_gain,
    gate_up_weight,
    down_weight,
):
    score_scale = 1.0 / math.sqrt(DH)
    owned = lengths.shape[0]
    local_rows = hidden_in.shape[1]
    kv_local = qkv_weight.shape[1]
    slot_count = qkv_weight.shape[2]
    group_size = slot_count - 2
    width = kv_local * slot_count * DH
    inputs = hidden_in.astype(jnp.float32)
    local_squares = jnp.sum(inputs * inputs, axis=1)
    scaled = (inputs * attn_gain.astype(jnp.float32)).astype(jnp.bfloat16)
    weight_flat = qkv_weight.reshape(local_rows, width)
    partial = jnp.dot(scaled, weight_flat, preferred_element_type=jnp.float32)
    summed = reduce_rows(jnp.concatenate([partial, local_squares[:, None]], axis=1), "wide")
    inv_rms = 1.0 / jnp.sqrt(summed[:, width] / D + norm_eps)
    projected = inv_rms[:, None] * summed[:, :width] + qkv_bias.reshape(width).astype(jnp.float32)
    projected = projected.reshape(owned, kv_local, slot_count, DH)
    cosine, sine_table = mrope_tables(positions)
    keys_rot = rotate(cache_keys.astype(jnp.float32), cosine[:, None], sine_table[:, None]).astype(
        jnp.bfloat16
    )
    new_position = jnp.take_along_axis(positions, lengths[:, None, None], axis=2)
    cos_new, sin_new = mrope_tables(new_position)
    query = rotate(projected[:, :, :group_size], cos_new[:, None], sin_new[:, None]).astype(
        jnp.bfloat16
    )
    key_new = rotate(projected[:, :, group_size], cos_new, sin_new).astype(jnp.bfloat16)
    value_new = projected[:, :, group_size + 1].astype(jnp.bfloat16)
    scores = (
        jnp.einsum("rgjd,rgsd->rgjs", query, keys_rot, preferred_element_type=jnp.float32)
        * score_scale
    )
    own_score = (
        jnp.sum(query.astype(jnp.float32) * key_new.astype(jnp.float32)[:, :, None, :], axis=3)
        * score_scale
    )
    valid_slot = jnp.arange(CACHE)[None, None, None, :] < lengths[:, None, None, None]
    row_max = jnp.maximum(jnp.max(jnp.where(valid_slot, scores, -jnp.inf), axis=3), own_score)
    probabilities = jnp.where(valid_slot, jnp.exp(scores - row_max[..., None]), 0.0)
    own_prob = jnp.exp(own_score - row_max)
    totals = jnp.sum(probabilities, axis=3) + own_prob
    probs_rounded = probabilities.astype(jnp.bfloat16)
    own_rounded = own_prob.astype(jnp.bfloat16).astype(jnp.float32)
    weighted = jnp.einsum(
        "rgjs,rgsd->rgjd", probs_rounded, cache_values, preferred_element_type=jnp.float32
    )
    weighted = weighted + own_rounded[..., None] * value_new.astype(jnp.float32)[:, :, None, :]
    attended = (
        (weighted / totals[..., None])
        .astype(jnp.bfloat16)
        .reshape(owned, kv_local * group_size * DH)
    )
    head_partial = jnp.dot(
        gather_rows(attended, "wide"),
        out_weight,
        preferred_element_type=jnp.float32,
    )
    attn_out = sum_all(head_partial, "narrow")
    residual = (inputs + attn_out).astype(jnp.bfloat16)
    resid_float = residual.astype(jnp.float32)
    resid_squares = jnp.sum(resid_float * resid_float, axis=1)
    scaled2 = (resid_float * mlp_gain.astype(jnp.float32)).astype(jnp.bfloat16)
    hidden_local = gate_up_weight.shape[2]
    gate_up_flat = gate_up_weight.reshape(local_rows, 2 * hidden_local)
    partial2 = jnp.dot(scaled2, gate_up_flat, preferred_element_type=jnp.float32)
    squares_hi = resid_squares.astype(jnp.bfloat16)
    squares_lo = (resid_squares - squares_hi.astype(jnp.float32)).astype(jnp.bfloat16)
    sent2 = jnp.concatenate(
        [partial2.astype(jnp.bfloat16), squares_hi[:, None], squares_lo[:, None]], axis=1
    )
    n_wide = lax.axis_size("wide")
    received2 = lax.all_to_all(
        sent2.reshape(n_wide, sent2.shape[0] // n_wide, sent2.shape[1]), "wide", 0, 0, tiled=False
    )
    summed2 = jnp.sum(received2.astype(jnp.float32), axis=0)
    total_squares2 = summed2[:, 2 * hidden_local] + summed2[:, 2 * hidden_local + 1]
    inv_rms2 = 1.0 / jnp.sqrt(total_squares2 / D + norm_eps)
    gate_up = summed2[:, : 2 * hidden_local] * inv_rms2[:, None]
    hidden = (jax.nn.silu(gate_up[:, :hidden_local]) * gate_up[:, hidden_local:]).astype(
        jnp.bfloat16
    )
    down_partial = jnp.dot(gather_rows(hidden, "wide"), down_weight, preferred_element_type=jnp.float32)
    mlp_out = sum_all(down_partial, "narrow")
    return (resid_float + mlp_out).astype(jnp.bfloat16)


def solution(mesh):
    in_specs = (
        P(None, "wide"),
        P("wide"),
        P("wide", "narrow", None, None),
        P("narrow", None, None),
        P("wide", "narrow", None, None),
        P("wide", "narrow", None, None),
        P("wide", None, None),
        P("wide"),
        P("narrow", "wide"),
        P("wide"),
        P("wide", None, "narrow"),
        P("narrow", "wide"),
    )
    out_specs = P(None, "wide")
    return jax.shard_map(local, mesh=mesh, in_specs=in_specs, out_specs=out_specs, check_vma=False)
```

```python
import math

import jax
import jax.numpy as jnp
from jax import lax
from jax.sharding import PartitionSpec as P

D = 8192
DH = 128
CACHE = 4096


norm_eps = 1e-06
rope_base = 1000000.0


def mrope_tables(position):
    half_width = DH // 2
    pair_index = jnp.arange(half_width)
    inv_freq = jnp.exp(pair_index.astype(jnp.float32) * (-2.0 * math.log(rope_base) / DH))
    component = (pair_index >= DH // 8).astype(jnp.int32) + (
        pair_index >= DH // 8 + 3 * DH // 16
    ).astype(jnp.int32)
    pos_float = position.astype(jnp.float32)
    chosen = jnp.where(
        component == 0,
        pos_float[..., 0, :, None],
        jnp.where(component == 1, pos_float[..., 1, :, None], pos_float[..., 2, :, None]),
    )
    angles = chosen * inv_freq
    return (jnp.cos(angles), jnp.sin(angles))


def rotate(values, cosine, sine_table):
    half_width = values.shape[-1] // 2
    leading = values[..., :half_width]
    trailing = values[..., half_width:]
    return jnp.concatenate(
        [leading * cosine - trailing * sine_table, trailing * cosine + leading * sine_table],
        axis=-1,
    )


def reduce_rows(x, axis):
    n = lax.axis_size(axis)
    blocks = x.reshape(n, x.shape[0] // n, x.shape[1])
    return jnp.sum(lax.all_to_all(blocks, axis, 0, 0, tiled=False), axis=0)


def gather_rows(x, axis):
    n = lax.axis_size(axis)
    copies = jnp.broadcast_to(x[None], (n,) + x.shape)
    return lax.all_to_all(copies, axis, 0, 0, tiled=False).reshape(n * x.shape[0], x.shape[1])


def sum_all(x, axis):
    n = lax.axis_size(axis)
    x = x + lax.ppermute(x, axis, [(i, i ^ 1) for i in range(n)])
    groups = n // 2
    if groups == 4:
        def shifted(k):
            return lax.ppermute(
                x, axis, [(i, ((i // 2 + k) % groups) * 2 + i % 2) for i in range(n)]
            )

        return (x + shifted(2)) + (shifted(1) + shifted(3))
    step = 2
    while step < n:
        x = x + lax.ppermute(x, axis, [(i, i ^ step) for i in range(n)])
        step *= 2
    return x


def local(
    hidden_in,
    attn_gain,
    qkv_weight,
    qkv_bias,
    cache_keys,
    cache_values,
    positions,
    lengths,
    out_weight,
    mlp_gain,
    gate_up_weight,
    down_weight,
):
    score_scale = 1.0 / math.sqrt(DH)
    owned = lengths.shape[0]
    local_rows = hidden_in.shape[1]
    kv_local = qkv_weight.shape[1]
    slot_count = qkv_weight.shape[2]
    group_size = slot_count - 2
    width = kv_local * slot_count * DH
    inputs = hidden_in.astype(jnp.float32)
    local_squares = jnp.sum(inputs * inputs, axis=1)
    scaled = (inputs * attn_gain.astype(jnp.float32)).astype(jnp.bfloat16)
    weight_flat = qkv_weight.reshape(local_rows, width)
    partial = jnp.dot(scaled, weight_flat, preferred_element_type=jnp.float32)
    summed = reduce_rows(jnp.concatenate([partial, local_squares[:, None]], axis=1), "wide")
    inv_rms = 1.0 / jnp.sqrt(summed[:, width] / D + norm_eps)
    projected = inv_rms[:, None] * summed[:, :width] + qkv_bias.reshape(width).astype(jnp.float32)
    projected = projected.reshape(owned, kv_local, slot_count, DH)
    cosine, sine_table = mrope_tables(positions)
    keys_rot = rotate(cache_keys.astype(jnp.float32), cosine[:, None], sine_table[:, None]).astype(
        jnp.bfloat16
    )
    new_position = jnp.take_along_axis(positions, lengths[:, None, None], axis=2)
    cos_new, sin_new = mrope_tables(new_position)
    query = rotate(projected[:, :, :group_size], cos_new[:, None], sin_new[:, None]).astype(
        jnp.bfloat16
    )
    key_new = rotate(projected[:, :, group_size], cos_new, sin_new).astype(jnp.bfloat16)
    value_new = projected[:, :, group_size + 1].astype(jnp.bfloat16)
    scores = (
        jnp.einsum("rgjd,rgsd->rgjs", query, keys_rot, preferred_element_type=jnp.float32)
        * score_scale
    )
    own_score = (
        jnp.sum(query.astype(jnp.float32) * key_new.astype(jnp.float32)[:, :, None, :], axis=3)
        * score_scale
    )
    valid_slot = jnp.arange(CACHE)[None, None, None, :] < lengths[:, None, None, None]
    row_max = jnp.maximum(jnp.max(jnp.where(valid_slot, scores, -jnp.inf), axis=3), own_score)
    probabilities = jnp.where(valid_slot, jnp.exp(scores - row_max[..., None]), 0.0)
    own_prob = jnp.exp(own_score - row_max)
    totals = jnp.sum(probabilities, axis=3) + own_prob
    probs_rounded = probabilities.astype(jnp.bfloat16)
    own_rounded = own_prob.astype(jnp.bfloat16).astype(jnp.float32)
    weighted = jnp.einsum(
        "rgjs,rgsd->rgjd", probs_rounded, cache_values, preferred_element_type=jnp.float32
    )
    weighted = weighted + own_rounded[..., None] * value_new.astype(jnp.float32)[:, :, None, :]
    attended = (
        (weighted / totals[..., None])
        .astype(jnp.bfloat16)
        .reshape(owned, kv_local * group_size * DH)
    )
    head_partial = jnp.dot(
        gather_rows(attended, "wide"),
        out_weight,
        preferred_element_type=jnp.float32,
    )
    attn_out = sum_all(head_partial, "narrow")
    residual = (inputs + attn_out).astype(jnp.bfloat16)
    resid_float = residual.astype(jnp.float32)
    resid_squares = jnp.sum(resid_float * resid_float, axis=1)
    scaled2 = (resid_float * mlp_gain.astype(jnp.float32)).astype(jnp.bfloat16)
    hidden_local = gate_up_weight.shape[2]
    gate_up_flat = gate_up_weight.reshape(local_rows, 2 * hidden_local)
    partial2 = jnp.dot(scaled2, gate_up_flat, preferred_element_type=jnp.float32)
    squares_hi = resid_squares.astype(jnp.bfloat16)
    squares_lo = (resid_squares - squares_hi.astype(jnp.float32)).astype(jnp.bfloat16)
    sent2 = jnp.concatenate(
        [partial2.astype(jnp.bfloat16), squares_hi[:, None], squares_lo[:, None]], axis=1
    )
    n_wide = lax.axis_size("wide")
    received2 = lax.all_to_all(
        sent2.reshape(n_wide, sent2.shape[0] // n_wide, sent2.shape[1]), "wide", 0, 0, tiled=False
    )
    summed2 = jnp.sum(received2.astype(jnp.float32), axis=0)
    total_squares2 = summed2[:, 2 * hidden_local] + summed2[:, 2 * hidden_local + 1]
    inv_rms2 = 1.0 / jnp.sqrt(total_squares2 / D + norm_eps)
    gate_up = summed2[:, : 2 * hidden_local] * inv_rms2[:, None]
    hidden = (jax.nn.silu(gate_up[:, :hidden_local]) * gate_up[:, hidden_local:]).astype(
        jnp.bfloat16
    )
    down_partial = jnp.dot(gather_rows(hidden, "wide"), down_weight, preferred_element_type=jnp.float32)
    mlp_out = sum_all(down_partial, "narrow")
    return (resid_float + mlp_out).astype(jnp.bfloat16)


def solution(mesh):
    in_specs = (
        P(None, "wide"),
        P("wide"),
        P("wide", "narrow", None, None),
        P("narrow", None, None),
        P("wide", "narrow", None, None),
        P("wide", "narrow", None, None),
        P("wide", None, None),
        P("wide"),
        P("narrow", "wide"),
        P("wide"),
        P("wide", None, "narrow"),
        P("narrow", "wide"),
    )
    out_specs = P(None, "wide")
    return jax.shard_map(local, mesh=mesh, in_specs=in_specs, out_specs=out_specs, check_vma=False)
```

```python
import math

import jax
import jax.numpy as jnp
from jax import lax
from jax.sharding import PartitionSpec as P

D = 8192
DH = 128
CACHE = 4096


norm_eps = 1e-06
rope_base = 1000000.0


def mrope_tables(position):
    half_width = DH // 2
    pair_index = jnp.arange(half_width)
    inv_freq = jnp.exp(pair_index.astype(jnp.float32) * (-2.0 * math.log(rope_base) / DH))
    component = (pair_index >= DH // 8).astype(jnp.int32) + (
        pair_index >= DH // 8 + 3 * DH // 16
    ).astype(jnp.int32)
    pos_float = position.astype(jnp.float32)
    chosen = jnp.where(
        component == 0,
        pos_float[..., 0, :, None],
        jnp.where(component == 1, pos_float[..., 1, :, None], pos_float[..., 2, :, None]),
    )
    angles = chosen * inv_freq
    return (jnp.cos(angles), jnp.sin(angles))


def rotate(values, cosine, sine_table):
    half_width = values.shape[-1] // 2
    leading = values[..., :half_width]
    trailing = values[..., half_width:]
    return jnp.concatenate(
        [leading * cosine - trailing * sine_table, trailing * cosine + leading * sine_table],
        axis=-1,
    )


def reduce_rows(x, axis):
    n = lax.axis_size(axis)
    blocks = x.reshape(n, x.shape[0] // n, x.shape[1])
    return jnp.sum(lax.all_to_all(blocks, axis, 0, 0, tiled=False), axis=0)


def gather_rows(x, axis):
    n = lax.axis_size(axis)
    copies = jnp.broadcast_to(x[None], (n,) + x.shape)
    return lax.all_to_all(copies, axis, 0, 0, tiled=False).reshape(n * x.shape[0], x.shape[1])


def sum_all(x, axis):
    n = lax.axis_size(axis)
    x = x + lax.ppermute(x, axis, [(i, i ^ 1) for i in range(n)])
    groups = n // 2
    if groups == 4:
        def shifted(k):
            return lax.ppermute(
                x, axis, [(i, ((i // 2 + k) % groups) * 2 + i % 2) for i in range(n)]
            )

        return (x + shifted(2)) + (shifted(1) + shifted(3))
    step = 2
    while step < n:
        x = x + lax.ppermute(x, axis, [(i, i ^ step) for i in range(n)])
        step *= 2
    return x


def local(
    hidden_in,
    attn_gain,
    qkv_weight,
    qkv_bias,
    cache_keys,
    cache_values,
    positions,
    lengths,
    out_weight,
    mlp_gain,
    gate_up_weight,
    down_weight,
):
    score_scale = 1.0 / math.sqrt(DH)
    owned = lengths.shape[0]
    local_rows = hidden_in.shape[1]
    kv_local = qkv_weight.shape[1]
    slot_count = qkv_weight.shape[2]
    group_size = slot_count - 2
    width = kv_local * slot_count * DH
    inputs = hidden_in.astype(jnp.float32)
    local_squares = jnp.sum(inputs * inputs, axis=1)
    scaled = (inputs * attn_gain.astype(jnp.float32)).astype(jnp.bfloat16)
    weight_flat = qkv_weight.reshape(local_rows, width)
    partial = jnp.dot(scaled, weight_flat, preferred_element_type=jnp.float32)
    summed = reduce_rows(jnp.concatenate([partial, local_squares[:, None]], axis=1), "wide")
    inv_rms = 1.0 / jnp.sqrt(summed[:, width] / D + norm_eps)
    projected = inv_rms[:, None] * summed[:, :width] + qkv_bias.reshape(width).astype(jnp.float32)
    projected = projected.reshape(owned, kv_local, slot_count, DH)
    cosine, sine_table = mrope_tables(positions)
    keys_rot = rotate(cache_keys.astype(jnp.float32), cosine[:, None], sine_table[:, None]).astype(
        jnp.bfloat16
    )
    new_position = jnp.take_along_axis(positions, lengths[:, None, None], axis=2)
    cos_new, sin_new = mrope_tables(new_position)
    query = rotate(projected[:, :, :group_size], cos_new[:, None], sin_new[:, None]).astype(
        jnp.bfloat16
    )
    key_new = rotate(projected[:, :, group_size], cos_new, sin_new).astype(jnp.bfloat16)
    value_new = projected[:, :, group_size + 1].astype(jnp.bfloat16)
    scores = (
        jnp.einsum("rgjd,rgsd->rgjs", query, keys_rot, preferred_element_type=jnp.float32)
        * score_scale
    )
    own_score = (
        jnp.sum(query.astype(jnp.float32) * key_new.astype(jnp.float32)[:, :, None, :], axis=3)
        * score_scale
    )
    valid_slot = jnp.arange(CACHE)[None, None, None, :] < lengths[:, None, None, None]
    row_max = jnp.maximum(jnp.max(jnp.where(valid_slot, scores, -jnp.inf), axis=3), own_score)
    probabilities = jnp.where(valid_slot, jnp.exp(scores - row_max[..., None]), 0.0)
    own_prob = jnp.exp(own_score - row_max)
    totals = jnp.sum(probabilities, axis=3) + own_prob
    probs_rounded = probabilities.astype(jnp.bfloat16)
    own_rounded = own_prob.astype(jnp.bfloat16).astype(jnp.float32)
    weighted = jnp.einsum(
        "rgjs,rgsd->rgjd", probs_rounded, cache_values, preferred_element_type=jnp.float32
    )
    weighted = weighted + own_rounded[..., None] * value_new.astype(jnp.float32)[:, :, None, :]
    attended = (
        (weighted / totals[..., None])
        .astype(jnp.bfloat16)
        .reshape(owned, kv_local * group_size * DH)
    )
    head_partial = jnp.dot(
        gather_rows(attended, "wide"),
        out_weight,
        preferred_element_type=jnp.float32,
    )
    attn_out = sum_all(head_partial, "narrow")
    residual = (inputs + attn_out).astype(jnp.bfloat16)
    resid_float = residual.astype(jnp.float32)
    resid_squares = jnp.sum(resid_float * resid_float, axis=1)
    scaled2 = (resid_float * mlp_gain.astype(jnp.float32)).astype(jnp.bfloat16)
    hidden_local = gate_up_weight.shape[2]
    gate_up_flat = gate_up_weight.reshape(local_rows, 2 * hidden_local)
    partial2 = jnp.dot(scaled2, gate_up_flat, preferred_element_type=jnp.float32)
    squares_hi = resid_squares.astype(jnp.bfloat16)
    squares_lo = (resid_squares - squares_hi.astype(jnp.float32)).astype(jnp.bfloat16)
    sent2 = jnp.pad(partial2.astype(jnp.bfloat16), ((0, 0), (0, 2)))
    sent2 = sent2.at[:, 2 * hidden_local].set(squares_hi)
    sent2 = sent2.at[:, 2 * hidden_local + 1].set(squares_lo)
    n_wide = lax.axis_size("wide")
    received2 = lax.all_to_all(
        sent2.reshape(n_wide, sent2.shape[0] // n_wide, sent2.shape[1]), "wide", 0, 0, tiled=False
    )
    summed2 = jnp.sum(received2.astype(jnp.float32), axis=0)
    total_squares2 = summed2[:, 2 * hidden_local] + summed2[:, 2 * hidden_local + 1]
    inv_rms2 = 1.0 / jnp.sqrt(total_squares2 / D + norm_eps)
    gate_up = summed2[:, : 2 * hidden_local] * inv_rms2[:, None]
    hidden = (jax.nn.silu(gate_up[:, :hidden_local]) * gate_up[:, hidden_local:]).astype(
        jnp.bfloat16
    )
    down_partial = jnp.dot(gather_rows(hidden, "wide"), down_weight, preferred_element_type=jnp.float32)
    mlp_out = sum_all(down_partial, "narrow")
    return (resid_float + mlp_out).astype(jnp.bfloat16)


def solution(mesh):
    in_specs = (
        P(None, "wide"),
        P("wide"),
        P("wide", "narrow", None, None),
        P("narrow", None, None),
        P("wide", "narrow", None, None),
        P("wide", "narrow", None, None),
        P("wide", None, None),
        P("wide"),
        P("narrow", "wide"),
        P("wide"),
        P("wide", None, "narrow"),
        P("narrow", "wide"),
    )
    out_specs = P(None, "wide")
    return jax.shard_map(local, mesh=mesh, in_specs=in_specs, out_specs=out_specs, check_vma=False)
```

```python
import math

import jax
import jax.numpy as jnp
from jax import lax
from jax.sharding import PartitionSpec as P

D = 8192
DH = 128
CACHE = 4096


norm_eps = 1e-06
rope_base = 1000000.0


def mrope_tables(position):
    half_width = DH // 2
    pair_index = jnp.arange(half_width)
    inv_freq = jnp.exp(pair_index.astype(jnp.float32) * (-2.0 * math.log(rope_base) / DH))
    component = (pair_index >= DH // 8).astype(jnp.int32) + (
        pair_index >= DH // 8 + 3 * DH // 16
    ).astype(jnp.int32)
    pos_float = position.astype(jnp.float32)
    chosen = jnp.where(
        component == 0,
        pos_float[..., 0, :, None],
        jnp.where(component == 1, pos_float[..., 1, :, None], pos_float[..., 2, :, None]),
    )
    angles = chosen * inv_freq
    return (jnp.cos(angles), jnp.sin(angles))


def rotate(values, cosine, sine_table):
    half_width = values.shape[-1] // 2
    leading = values[..., :half_width]
    trailing = values[..., half_width:]
    return jnp.concatenate(
        [leading * cosine - trailing * sine_table, trailing * cosine + leading * sine_table],
        axis=-1,
    )


def reduce_rows(x, axis):
    n = lax.axis_size(axis)
    blocks = x.reshape(n, x.shape[0] // n, x.shape[1])
    return jnp.sum(lax.all_to_all(blocks, axis, 0, 0, tiled=False), axis=0)


def gather_rows(x, axis):
    n = lax.axis_size(axis)
    copies = jnp.broadcast_to(x[None], (n,) + x.shape)
    return lax.all_to_all(copies, axis, 0, 0, tiled=False).reshape(n * x.shape[0], x.shape[1])


def sum_all(x, axis):
    n = lax.axis_size(axis)
    x = x + lax.ppermute(x, axis, [(i, i ^ 1) for i in range(n)])
    groups = n // 2
    if groups == 4:
        def shifted(k):
            return lax.ppermute(
                x, axis, [(i, ((i // 2 + k) % groups) * 2 + i % 2) for i in range(n)]
            )

        return (x + shifted(2)) + (shifted(1) + shifted(3))
    step = 2
    while step < n:
        x = x + lax.ppermute(x, axis, [(i, i ^ step) for i in range(n)])
        step *= 2
    return x


def local(
    hidden_in,
    attn_gain,
    qkv_weight,
    qkv_bias,
    cache_keys,
    cache_values,
    positions,
    lengths,
    out_weight,
    mlp_gain,
    gate_up_weight,
    down_weight,
):
    score_scale = 1.0 / math.sqrt(DH)
    owned = lengths.shape[0]
    local_rows = hidden_in.shape[1]
    kv_local = qkv_weight.shape[1]
    slot_count = qkv_weight.shape[2]
    group_size = slot_count - 2
    width = kv_local * slot_count * DH
    inputs = hidden_in.astype(jnp.float32)
    local_squares = jnp.sum(inputs * inputs, axis=1)
    scaled = (inputs * attn_gain.astype(jnp.float32)).astype(jnp.bfloat16)
    weight_flat = qkv_weight.reshape(local_rows, width)
    partial = jnp.dot(scaled, weight_flat, preferred_element_type=jnp.float32)
    summed = reduce_rows(jnp.concatenate([partial, local_squares[:, None]], axis=1), "wide")
    inv_rms = 1.0 / jnp.sqrt(summed[:, width] / D + norm_eps)
    projected = inv_rms[:, None] * summed[:, :width] + qkv_bias.reshape(width).astype(jnp.float32)
    projected = projected.reshape(owned, kv_local, slot_count, DH)
    cosine, sine_table = mrope_tables(positions)
    keys_rot = rotate(cache_keys.astype(jnp.float32), cosine[:, None], sine_table[:, None]).astype(
        jnp.bfloat16
    )
    at_new_slot = jnp.arange(CACHE)[None, None, :] == lengths[:, None, None]
    new_position = jnp.sum(jnp.where(at_new_slot, positions, 0), axis=2, keepdims=True)
    cos_new, sin_new = mrope_tables(new_position)
    query = rotate(projected[:, :, :group_size], cos_new[:, None], sin_new[:, None]).astype(
        jnp.bfloat16
    )
    key_new = rotate(projected[:, :, group_size], cos_new, sin_new).astype(jnp.bfloat16)
    value_new = projected[:, :, group_size + 1].astype(jnp.bfloat16)
    scores = (
        jnp.einsum("rgjd,rgsd->rgjs", query, keys_rot, preferred_element_type=jnp.float32)
        * score_scale
    )
    own_score = (
        jnp.sum(query.astype(jnp.float32) * key_new.astype(jnp.float32)[:, :, None, :], axis=3)
        * score_scale
    )
    valid_slot = jnp.arange(CACHE)[None, None, None, :] < lengths[:, None, None, None]
    row_max = jnp.maximum(jnp.max(jnp.where(valid_slot, scores, -jnp.inf), axis=3), own_score)
    probabilities = jnp.where(valid_slot, jnp.exp(scores - row_max[..., None]), 0.0)
    own_prob = jnp.exp(own_score - row_max)
    totals = jnp.sum(probabilities, axis=3) + own_prob
    probs_rounded = probabilities.astype(jnp.bfloat16)
    own_rounded = own_prob.astype(jnp.bfloat16).astype(jnp.float32)
    weighted = jnp.einsum(
        "rgjs,rgsd->rgjd", probs_rounded, cache_values, preferred_element_type=jnp.float32
    )
    weighted = weighted + own_rounded[..., None] * value_new.astype(jnp.float32)[:, :, None, :]
    attended = (
        (weighted / totals[..., None])
        .astype(jnp.bfloat16)
        .reshape(owned, kv_local * group_size * DH)
    )
    head_partial = jnp.dot(
        gather_rows(attended, "wide"),
        out_weight,
        preferred_element_type=jnp.float32,
    )
    attn_out = sum_all(head_partial, "narrow")
    residual = (inputs + attn_out).astype(jnp.bfloat16)
    resid_float = residual.astype(jnp.float32)
    resid_squares = jnp.sum(resid_float * resid_float, axis=1)
    scaled2 = (resid_float * mlp_gain.astype(jnp.float32)).astype(jnp.bfloat16)
    hidden_local = gate_up_weight.shape[2]
    gate_up_flat = gate_up_weight.reshape(local_rows, 2 * hidden_local)
    partial2 = jnp.dot(scaled2, gate_up_flat, preferred_element_type=jnp.float32)
    squares_hi = resid_squares.astype(jnp.bfloat16)
    squares_lo = (resid_squares - squares_hi.astype(jnp.float32)).astype(jnp.bfloat16)
    sent2 = jnp.pad(partial2.astype(jnp.bfloat16), ((0, 0), (0, 2)))
    sent2 = sent2.at[:, 2 * hidden_local].set(squares_hi)
    sent2 = sent2.at[:, 2 * hidden_local + 1].set(squares_lo)
    n_wide = lax.axis_size("wide")
    received2 = lax.all_to_all(
        sent2.reshape(n_wide, sent2.shape[0] // n_wide, sent2.shape[1]), "wide", 0, 0, tiled=False
    )
    summed2 = jnp.sum(received2.astype(jnp.float32), axis=0)
    total_squares2 = summed2[:, 2 * hidden_local] + summed2[:, 2 * hidden_local + 1]
    inv_rms2 = 1.0 / jnp.sqrt(total_squares2 / D + norm_eps)
    gate_up = summed2[:, : 2 * hidden_local] * inv_rms2[:, None]
    hidden = (jax.nn.silu(gate_up[:, :hidden_local]) * gate_up[:, hidden_local:]).astype(
        jnp.bfloat16
    )
    down_partial = jnp.dot(gather_rows(hidden, "wide"), down_weight, preferred_element_type=jnp.float32)
    mlp_out = sum_all(down_partial, "narrow")
    return (resid_float + mlp_out).astype(jnp.bfloat16)


def solution(mesh):
    in_specs = (
        P(None, "wide"),
        P("wide"),
        P("wide", "narrow", None, None),
        P("narrow", None, None),
        P("wide", "narrow", None, None),
        P("wide", "narrow", None, None),
        P("wide", None, None),
        P("wide"),
        P("narrow", "wide"),
        P("wide"),
        P("wide", None, "narrow"),
        P("narrow", "wide"),
    )
    out_specs = P(None, "wide")
    return jax.shard_map(local, mesh=mesh, in_specs=in_specs, out_specs=out_specs, check_vma=False)
```

```python
import math

import jax
import jax.numpy as jnp
from jax import lax
from jax.sharding import PartitionSpec as P

D = 8192
DH = 128
CACHE = 4096


norm_eps = 1e-06
rope_base = 1000000.0


def mrope_tables(position):
    half_width = DH // 2
    pair_index = jnp.arange(half_width)
    inv_freq = jnp.exp(pair_index.astype(jnp.float32) * (-2.0 * math.log(rope_base) / DH))
    component = (pair_index >= DH // 8).astype(jnp.int32) + (
        pair_index >= DH // 8 + 3 * DH // 16
    ).astype(jnp.int32)
    pos_float = position.astype(jnp.float32)
    chosen = jnp.where(
        component == 0,
        pos_float[..., 0, :, None],
        jnp.where(component == 1, pos_float[..., 1, :, None], pos_float[..., 2, :, None]),
    )
    angles = chosen * inv_freq
    return (jnp.cos(angles), jnp.sin(angles))


def rotate(values, cosine, sine_table):
    half_width = values.shape[-1] // 2
    leading = values[..., :half_width]
    trailing = values[..., half_width:]
    return jnp.concatenate(
        [leading * cosine - trailing * sine_table, trailing * cosine + leading * sine_table],
        axis=-1,
    )


def reduce_rows(x, axis):
    n = lax.axis_size(axis)
    blocks = x.reshape(n, x.shape[0] // n, x.shape[1])
    return jnp.sum(lax.all_to_all(blocks, axis, 0, 0, tiled=False), axis=0)


def gather_rows(x, axis):
    n = lax.axis_size(axis)
    copies = jnp.broadcast_to(x[None], (n,) + x.shape)
    return lax.all_to_all(copies, axis, 0, 0, tiled=False).reshape(n * x.shape[0], x.shape[1])


def sum_all(x, axis):
    n = lax.axis_size(axis)
    x = x + lax.ppermute(x, axis, [(i, i ^ 1) for i in range(n)])
    groups = n // 2
    if groups == 4:
        def shifted(k):
            return lax.ppermute(
                x, axis, [(i, ((i // 2 + k) % groups) * 2 + i % 2) for i in range(n)]
            )

        return (x + shifted(2)) + (shifted(1) + shifted(3))
    step = 2
    while step < n:
        x = x + lax.ppermute(x, axis, [(i, i ^ step) for i in range(n)])
        step *= 2
    return x


def local(
    hidden_in,
    attn_gain,
    qkv_weight,
    qkv_bias,
    cache_keys,
    cache_values,
    positions,
    lengths,
    out_weight,
    mlp_gain,
    gate_up_weight,
    down_weight,
):
    score_scale = 1.0 / math.sqrt(DH)
    owned = lengths.shape[0]
    local_rows = hidden_in.shape[1]
    kv_local = qkv_weight.shape[1]
    slot_count = qkv_weight.shape[2]
    group_size = slot_count - 2
    width = kv_local * slot_count * DH
    inputs = hidden_in.astype(jnp.float32)
    local_squares = jnp.sum(inputs * inputs, axis=1)
    scaled = (inputs * attn_gain.astype(jnp.float32)).astype(jnp.bfloat16)
    weight_flat = qkv_weight.reshape(local_rows, width)
    partial = jnp.dot(scaled, weight_flat, preferred_element_type=jnp.float32)
    summed = reduce_rows(jnp.concatenate([partial, local_squares[:, None]], axis=1), "wide")
    inv_rms = 1.0 / jnp.sqrt(summed[:, width] / D + norm_eps)
    projected = inv_rms[:, None] * summed[:, :width] + qkv_bias.reshape(width).astype(jnp.float32)
    projected = projected.reshape(owned, kv_local, slot_count, DH)
    cosine, sine_table = mrope_tables(positions)
    half_width = DH // 2
    keys_lead = cache_keys[..., :half_width].astype(jnp.float32)
    keys_trail = cache_keys[..., half_width:].astype(jnp.float32)
    cos_keys, sin_keys = cosine[:, None], sine_table[:, None]
    keys_rot = jnp.concatenate(
        [keys_lead * cos_keys - keys_trail * sin_keys, keys_trail * cos_keys + keys_lead * sin_keys],
        axis=-1,
    ).astype(jnp.bfloat16)
    at_new_slot = jnp.arange(CACHE)[None, None, :] == lengths[:, None, None]
    new_position = jnp.sum(jnp.where(at_new_slot, positions, 0), axis=2, keepdims=True)
    cos_new, sin_new = mrope_tables(new_position)
    query = rotate(projected[:, :, :group_size], cos_new[:, None], sin_new[:, None]).astype(
        jnp.bfloat16
    )
    key_new = rotate(projected[:, :, group_size], cos_new, sin_new).astype(jnp.bfloat16)
    value_new = projected[:, :, group_size + 1].astype(jnp.bfloat16)
    scores = (
        jnp.einsum("rgjd,rgsd->rgjs", query, keys_rot, preferred_element_type=jnp.float32)
        * score_scale
    )
    own_score = (
        jnp.sum(query.astype(jnp.float32) * key_new.astype(jnp.float32)[:, :, None, :], axis=3)
        * score_scale
    )
    valid_slot = jnp.arange(CACHE)[None, None, None, :] < lengths[:, None, None, None]
    row_max = jnp.maximum(jnp.max(jnp.where(valid_slot, scores, -jnp.inf), axis=3), own_score)
    probabilities = jnp.where(valid_slot, jnp.exp(scores - row_max[..., None]), 0.0)
    own_prob = jnp.exp(own_score - row_max)
    totals = jnp.sum(probabilities, axis=3) + own_prob
    probs_rounded = probabilities.astype(jnp.bfloat16)
    own_rounded = own_prob.astype(jnp.bfloat16).astype(jnp.float32)
    weighted = jnp.einsum(
        "rgjs,rgsd->rgjd", probs_rounded, cache_values, preferred_element_type=jnp.float32
    )
    weighted = weighted + own_rounded[..., None] * value_new.astype(jnp.float32)[:, :, None, :]
    attended = (
        (weighted / totals[..., None])
        .astype(jnp.bfloat16)
        .reshape(owned, kv_local * group_size * DH)
    )
    head_partial = jnp.dot(
        gather_rows(attended, "wide"),
        out_weight,
        preferred_element_type=jnp.float32,
    )
    attn_out = sum_all(head_partial, "narrow")
    residual = (inputs + attn_out).astype(jnp.bfloat16)
    resid_float = residual.astype(jnp.float32)
    resid_squares = jnp.sum(resid_float * resid_float, axis=1)
    scaled2 = (resid_float * mlp_gain.astype(jnp.float32)).astype(jnp.bfloat16)
    hidden_local = gate_up_weight.shape[2]
    gate_up_flat = gate_up_weight.reshape(local_rows, 2 * hidden_local)
    partial2 = jnp.dot(scaled2, gate_up_flat, preferred_element_type=jnp.float32)
    squares_hi = resid_squares.astype(jnp.bfloat16)
    squares_lo = (resid_squares - squares_hi.astype(jnp.float32)).astype(jnp.bfloat16)
    sent2 = jnp.pad(partial2.astype(jnp.bfloat16), ((0, 0), (0, 2)))
    sent2 = sent2.at[:, 2 * hidden_local].set(squares_hi)
    sent2 = sent2.at[:, 2 * hidden_local + 1].set(squares_lo)
    n_wide = lax.axis_size("wide")
    received2 = lax.all_to_all(
        sent2.reshape(n_wide, sent2.shape[0] // n_wide, sent2.shape[1]), "wide", 0, 0, tiled=False
    )
    summed2 = jnp.sum(received2.astype(jnp.float32), axis=0)
    total_squares2 = summed2[:, 2 * hidden_local] + summed2[:, 2 * hidden_local + 1]
    inv_rms2 = 1.0 / jnp.sqrt(total_squares2 / D + norm_eps)
    gate_up = summed2[:, : 2 * hidden_local] * inv_rms2[:, None]
    hidden = (jax.nn.silu(gate_up[:, :hidden_local]) * gate_up[:, hidden_local:]).astype(
        jnp.bfloat16
    )
    down_partial = jnp.dot(gather_rows(hidden, "wide"), down_weight, preferred_element_type=jnp.float32)
    mlp_out = sum_all(down_partial, "narrow")
    return (resid_float + mlp_out).astype(jnp.bfloat16)


def solution(mesh):
    in_specs = (
        P(None, "wide"),
        P("wide"),
        P("wide", "narrow", None, None),
        P("narrow", None, None),
        P("wide", "narrow", None, None),
        P("wide", "narrow", None, None),
        P("wide", None, None),
        P("wide"),
        P("narrow", "wide"),
        P("wide"),
        P("wide", None, "narrow"),
        P("narrow", "wide"),
    )
    out_specs = P(None, "wide")
    return jax.shard_map(local, mesh=mesh, in_specs=in_specs, out_specs=out_specs, check_vma=False)
```

```python
import math

import jax
import jax.numpy as jnp
from jax import lax
from jax.sharding import PartitionSpec as P

D = 8192
DH = 128
CACHE = 4096


norm_eps = 1e-06
rope_base = 1000000.0


def cos_sin(angle):
    k = jnp.round(angle * 0.6366197723675814)
    r = ((angle - k * 1.5703125) - k * 4.837512969970703125e-4) - k * 7.54978995489188216e-8
    z = r * r
    s = r + r * z * (-1.6666654611e-1 + z * (8.3321608736e-3 + z * -1.9515295891e-4))
    c = 1.0 - 0.5 * z + z * z * (
        4.166664568298827e-2 + z * (-1.388731625493765e-3 + z * 2.443315711809948e-5)
    )
    quadrant = k - 4.0 * jnp.floor(k * 0.25)
    odd = (quadrant == 1.0) | (quadrant == 3.0)
    cos_sign = jnp.where((quadrant == 1.0) | (quadrant == 2.0), -1.0, 1.0)
    sin_sign = jnp.where(quadrant >= 2.0, -1.0, 1.0)
    return cos_sign * jnp.where(odd, s, c), sin_sign * jnp.where(odd, c, s)


def mrope_tables(position):
    half_width = DH // 2
    pair_index = jnp.arange(half_width)
    inv_freq = jnp.exp(pair_index.astype(jnp.float32) * (-2.0 * math.log(rope_base) / DH))
    component = (pair_index >= DH // 8).astype(jnp.int32) + (
        pair_index >= DH // 8 + 3 * DH // 16
    ).astype(jnp.int32)
    pos_float = position.astype(jnp.float32)
    chosen = jnp.where(
        component == 0,
        pos_float[..., 0, :, None],
        jnp.where(component == 1, pos_float[..., 1, :, None], pos_float[..., 2, :, None]),
    )
    angles = chosen * inv_freq
    return cos_sin(angles)


def rotate(values, cosine, sine_table):
    half_width = values.shape[-1] // 2
    leading = values[..., :half_width]
    trailing = values[..., half_width:]
    return jnp.concatenate(
        [leading * cosine - trailing * sine_table, trailing * cosine + leading * sine_table],
        axis=-1,
    )


def reduce_rows(x, axis):
    n = lax.axis_size(axis)
    blocks = x.reshape(n, x.shape[0] // n, x.shape[1])
    return jnp.sum(lax.all_to_all(blocks, axis, 0, 0, tiled=False), axis=0)


def gather_rows(x, axis):
    n = lax.axis_size(axis)
    copies = jnp.broadcast_to(x[None], (n,) + x.shape)
    return lax.all_to_all(copies, axis, 0, 0, tiled=False).reshape(n * x.shape[0], x.shape[1])


def sum_all(x, axis):
    n = lax.axis_size(axis)
    x = x + lax.ppermute(x, axis, [(i, i ^ 1) for i in range(n)])
    groups = n // 2
    if groups == 4:
        def shifted(k):
            return lax.ppermute(
                x, axis, [(i, ((i // 2 + k) % groups) * 2 + i % 2) for i in range(n)]
            )

        return (x + shifted(2)) + (shifted(1) + shifted(3))
    step = 2
    while step < n:
        x = x + lax.ppermute(x, axis, [(i, i ^ step) for i in range(n)])
        step *= 2
    return x


def local(
    hidden_in,
    attn_gain,
    qkv_weight,
    qkv_bias,
    cache_keys,
    cache_values,
    positions,
    lengths,
    out_weight,
    mlp_gain,
    gate_up_weight,
    down_weight,
):
    score_scale = 1.0 / math.sqrt(DH)
    owned = lengths.shape[0]
    local_rows = hidden_in.shape[1]
    kv_local = qkv_weight.shape[1]
    slot_count = qkv_weight.shape[2]
    group_size = slot_count - 2
    width = kv_local * slot_count * DH
    inputs = hidden_in.astype(jnp.float32)
    local_squares = jnp.sum(inputs * inputs, axis=1)
    scaled = (inputs * attn_gain.astype(jnp.float32)).astype(jnp.bfloat16)
    weight_flat = qkv_weight.reshape(local_rows, width)
    partial = jnp.dot(scaled, weight_flat, preferred_element_type=jnp.float32)
    summed = reduce_rows(jnp.concatenate([partial, local_squares[:, None]], axis=1), "wide")
    inv_rms = 1.0 / jnp.sqrt(summed[:, width] / D + norm_eps)
    projected = inv_rms[:, None] * summed[:, :width] + qkv_bias.reshape(width).astype(jnp.float32)
    projected = projected.reshape(owned, kv_local, slot_count, DH)
    cosine, sine_table = mrope_tables(positions)
    half_width = DH // 2
    keys_lead = cache_keys[..., :half_width].astype(jnp.float32)
    keys_trail = cache_keys[..., half_width:].astype(jnp.float32)
    cos_keys, sin_keys = cosine[:, None], sine_table[:, None]
    keys_rot = jnp.concatenate(
        [keys_lead * cos_keys - keys_trail * sin_keys, keys_trail * cos_keys + keys_lead * sin_keys],
        axis=-1,
    ).astype(jnp.bfloat16)
    at_new_slot = jnp.arange(CACHE)[None, None, :] == lengths[:, None, None]
    new_position = jnp.sum(jnp.where(at_new_slot, positions, 0), axis=2, keepdims=True)
    cos_new, sin_new = mrope_tables(new_position)
    query = rotate(projected[:, :, :group_size], cos_new[:, None], sin_new[:, None]).astype(
        jnp.bfloat16
    )
    key_new = rotate(projected[:, :, group_size], cos_new, sin_new).astype(jnp.bfloat16)
    value_new = projected[:, :, group_size + 1].astype(jnp.bfloat16)
    scores = (
        jnp.einsum("rgjd,rgsd->rgjs", query, keys_rot, preferred_element_type=jnp.float32)
        * score_scale
    )
    own_score = (
        jnp.sum(query.astype(jnp.float32) * key_new.astype(jnp.float32)[:, :, None, :], axis=3)
        * score_scale
    )
    valid_slot = jnp.arange(CACHE)[None, None, None, :] < lengths[:, None, None, None]
    row_max = jnp.maximum(jnp.max(jnp.where(valid_slot, scores, -jnp.inf), axis=3), own_score)
    probabilities = jnp.where(valid_slot, jnp.exp(scores - row_max[..., None]), 0.0)
    own_prob = jnp.exp(own_score - row_max)
    totals = jnp.sum(probabilities, axis=3) + own_prob
    probs_rounded = probabilities.astype(jnp.bfloat16)
    own_rounded = own_prob.astype(jnp.bfloat16).astype(jnp.float32)
    weighted = jnp.einsum(
        "rgjs,rgsd->rgjd", probs_rounded, cache_values, preferred_element_type=jnp.float32
    )
    weighted = weighted + own_rounded[..., None] * value_new.astype(jnp.float32)[:, :, None, :]
    attended = (
        (weighted / totals[..., None])
        .astype(jnp.bfloat16)
        .reshape(owned, kv_local * group_size * DH)
    )
    head_partial = jnp.dot(
        gather_rows(attended, "wide"),
        out_weight,
        preferred_element_type=jnp.float32,
    )
    attn_out = sum_all(head_partial, "narrow")
    residual = (inputs + attn_out).astype(jnp.bfloat16)
    resid_float = residual.astype(jnp.float32)
    resid_squares = jnp.sum(resid_float * resid_float, axis=1)
    scaled2 = (resid_float * mlp_gain.astype(jnp.float32)).astype(jnp.bfloat16)
    hidden_local = gate_up_weight.shape[2]
    gate_up_flat = gate_up_weight.reshape(local_rows, 2 * hidden_local)
    partial2 = jnp.dot(scaled2, gate_up_flat, preferred_element_type=jnp.float32)
    squares_hi = resid_squares.astype(jnp.bfloat16)
    squares_lo = (resid_squares - squares_hi.astype(jnp.float32)).astype(jnp.bfloat16)
    sent2 = jnp.pad(partial2.astype(jnp.bfloat16), ((0, 0), (0, 2)))
    sent2 = sent2.at[:, 2 * hidden_local].set(squares_hi)
    sent2 = sent2.at[:, 2 * hidden_local + 1].set(squares_lo)
    n_wide = lax.axis_size("wide")
    received2 = lax.all_to_all(
        sent2.reshape(n_wide, sent2.shape[0] // n_wide, sent2.shape[1]), "wide", 0, 0, tiled=False
    )
    summed2 = jnp.sum(received2.astype(jnp.float32), axis=0)
    total_squares2 = summed2[:, 2 * hidden_local] + summed2[:, 2 * hidden_local + 1]
    inv_rms2 = 1.0 / jnp.sqrt(total_squares2 / D + norm_eps)
    gate_up = summed2[:, : 2 * hidden_local] * inv_rms2[:, None]
    hidden = (jax.nn.silu(gate_up[:, :hidden_local]) * gate_up[:, hidden_local:]).astype(
        jnp.bfloat16
    )
    down_partial = jnp.dot(gather_rows(hidden, "wide"), down_weight, preferred_element_type=jnp.float32)
    mlp_out = sum_all(down_partial, "narrow")
    return (resid_float + mlp_out).astype(jnp.bfloat16)


def solution(mesh):
    in_specs = (
        P(None, "wide"),
        P("wide"),
        P("wide", "narrow", None, None),
        P("narrow", None, None),
        P("wide", "narrow", None, None),
        P("wide", "narrow", None, None),
        P("wide", None, None),
        P("wide"),
        P("narrow", "wide"),
        P("wide"),
        P("wide", None, "narrow"),
        P("narrow", "wide"),
    )
    out_specs = P(None, "wide")
    return jax.shard_map(local, mesh=mesh, in_specs=in_specs, out_specs=out_specs, check_vma=False)
```

```python
import math

import jax
import jax.numpy as jnp
from jax import lax
from jax.sharding import PartitionSpec as P

D = 8192
DH = 128
CACHE = 4096


norm_eps = 1e-06
rope_base = 1000000.0


def cos_sin(angle):
    k = jnp.round(angle * 0.6366197723675814)
    r = ((angle - k * 1.5703125) - k * 4.837512969970703125e-4) - k * 7.54978995489188216e-8
    z = r * r
    s = r + r * z * (-1.6666654611e-1 + z * (8.3321608736e-3 + z * -1.9515295891e-4))
    c = 1.0 - 0.5 * z + z * z * (
        4.166664568298827e-2 + z * (-1.388731625493765e-3 + z * 2.443315711809948e-5)
    )
    quadrant = k - 4.0 * jnp.floor(k * 0.25)
    odd = (quadrant == 1.0) | (quadrant == 3.0)
    cos_sign = jnp.where((quadrant == 1.0) | (quadrant == 2.0), -1.0, 1.0)
    sin_sign = jnp.where(quadrant >= 2.0, -1.0, 1.0)
    return cos_sign * jnp.where(odd, s, c), sin_sign * jnp.where(odd, c, s)


def mrope_tables(position):
    half_width = DH // 2
    pair_index = jnp.arange(half_width)
    inv_freq = jnp.exp(pair_index.astype(jnp.float32) * (-2.0 * math.log(rope_base) / DH))
    component = (pair_index >= DH // 8).astype(jnp.int32) + (
        pair_index >= DH // 8 + 3 * DH // 16
    ).astype(jnp.int32)
    pos_float = position.astype(jnp.float32)
    chosen = jnp.where(
        component == 0,
        pos_float[..., 0, :, None],
        jnp.where(component == 1, pos_float[..., 1, :, None], pos_float[..., 2, :, None]),
    )
    angles = chosen * inv_freq
    return cos_sin(angles)


def rotate(values, cosine, sine_table):
    half_width = values.shape[-1] // 2
    leading = values[..., :half_width]
    trailing = values[..., half_width:]
    return jnp.concatenate(
        [leading * cosine - trailing * sine_table, trailing * cosine + leading * sine_table],
        axis=-1,
    )


def reduce_rows(x, axis):
    n = lax.axis_size(axis)
    blocks = x.reshape(n, x.shape[0] // n, x.shape[1])
    return jnp.sum(lax.all_to_all(blocks, axis, 0, 0, tiled=False), axis=0)


def gather_rows(x, axis):
    n = lax.axis_size(axis)
    copies = jnp.broadcast_to(x[None], (n,) + x.shape)
    return lax.all_to_all(copies, axis, 0, 0, tiled=False).reshape(n * x.shape[0], x.shape[1])


def sum_all(x, axis):
    n = lax.axis_size(axis)
    x = x + lax.ppermute(x, axis, [(i, i ^ 1) for i in range(n)])
    groups = n // 2
    if groups == 4:
        def shifted(k):
            return lax.ppermute(
                x, axis, [(i, ((i // 2 + k) % groups) * 2 + i % 2) for i in range(n)]
            )

        return (x + shifted(2)) + (shifted(1) + shifted(3))
    step = 2
    while step < n:
        x = x + lax.ppermute(x, axis, [(i, i ^ step) for i in range(n)])
        step *= 2
    return x


def local(
    hidden_in,
    attn_gain,
    qkv_weight,
    qkv_bias,
    cache_keys,
    cache_values,
    positions,
    lengths,
    out_weight,
    mlp_gain,
    gate_up_weight,
    down_weight,
):
    score_scale = 1.0 / math.sqrt(DH)
    owned = lengths.shape[0]
    local_rows = hidden_in.shape[1]
    kv_local = qkv_weight.shape[1]
    slot_count = qkv_weight.shape[2]
    group_size = slot_count - 2
    width = kv_local * slot_count * DH
    inputs = hidden_in.astype(jnp.float32)
    local_squares = jnp.sum(inputs * inputs, axis=1)
    scaled = (inputs * attn_gain.astype(jnp.float32)).astype(jnp.bfloat16)
    weight_flat = qkv_weight.reshape(local_rows, width)
    weight_by_slot = qkv_weight.reshape(local_rows, slot_count * kv_local, DH).transpose(1, 0, 2)
    partial = lax.dot_general(
        jnp.broadcast_to(scaled[None], (slot_count * kv_local,) + scaled.shape),
        weight_by_slot,
        (((2,), (1,)), ((0,), (0,))),
        preferred_element_type=jnp.float32,
    )
    partial = partial.transpose(1, 0, 2).reshape(scaled.shape[0], width)
    summed = reduce_rows(jnp.concatenate([partial, local_squares[:, None]], axis=1), "wide")
    inv_rms = 1.0 / jnp.sqrt(summed[:, width] / D + norm_eps)
    projected = inv_rms[:, None] * summed[:, :width] + qkv_bias.reshape(width).astype(jnp.float32)
    projected = projected.reshape(owned, kv_local, slot_count, DH)
    cosine, sine_table = mrope_tables(positions)
    half_width = DH // 2
    keys_lead = cache_keys[..., :half_width].astype(jnp.float32)
    keys_trail = cache_keys[..., half_width:].astype(jnp.float32)
    cos_keys, sin_keys = cosine[:, None], sine_table[:, None]
    keys_rot = jnp.concatenate(
        [keys_lead * cos_keys - keys_trail * sin_keys, keys_trail * cos_keys + keys_lead * sin_keys],
        axis=-1,
    ).astype(jnp.bfloat16)
    at_new_slot = jnp.arange(CACHE)[None, None, :] == lengths[:, None, None]
    new_position = jnp.sum(jnp.where(at_new_slot, positions, 0), axis=2, keepdims=True)
    cos_new, sin_new = mrope_tables(new_position)
    query = rotate(projected[:, :, :group_size], cos_new[:, None], sin_new[:, None]).astype(
        jnp.bfloat16
    )
    key_new = rotate(projected[:, :, group_size], cos_new, sin_new).astype(jnp.bfloat16)
    value_new = projected[:, :, group_size + 1].astype(jnp.bfloat16)
    scores = (
        jnp.einsum("rgjd,rgsd->rgjs", query, keys_rot, preferred_element_type=jnp.float32)
        * score_scale
    )
    own_score = (
        jnp.sum(query.astype(jnp.float32) * key_new.astype(jnp.float32)[:, :, None, :], axis=3)
        * score_scale
    )
    valid_slot = jnp.arange(CACHE)[None, None, None, :] < lengths[:, None, None, None]
    row_max = jnp.maximum(jnp.max(jnp.where(valid_slot, scores, -jnp.inf), axis=3), own_score)
    probabilities = jnp.where(valid_slot, jnp.exp(scores - row_max[..., None]), 0.0)
    own_prob = jnp.exp(own_score - row_max)
    totals = jnp.sum(probabilities, axis=3) + own_prob
    probs_rounded = probabilities.astype(jnp.bfloat16)
    own_rounded = own_prob.astype(jnp.bfloat16).astype(jnp.float32)
    weighted = jnp.einsum(
        "rgjs,rgsd->rgjd", probs_rounded, cache_values, preferred_element_type=jnp.float32
    )
    weighted = weighted + own_rounded[..., None] * value_new.astype(jnp.float32)[:, :, None, :]
    attended = (
        (weighted / totals[..., None])
        .astype(jnp.bfloat16)
        .reshape(owned, kv_local * group_size * DH)
    )
    head_partial = jnp.dot(
        gather_rows(attended, "wide"),
        out_weight,
        preferred_element_type=jnp.float32,
    )
    attn_out = sum_all(head_partial, "narrow")
    residual = (inputs + attn_out).astype(jnp.bfloat16)
    resid_float = residual.astype(jnp.float32)
    resid_squares = jnp.sum(resid_float * resid_float, axis=1)
    scaled2 = (resid_float * mlp_gain.astype(jnp.float32)).astype(jnp.bfloat16)
    hidden_local = gate_up_weight.shape[2]
    gate_up_flat = gate_up_weight.reshape(local_rows, 2 * hidden_local)
    partial2 = jnp.dot(scaled2, gate_up_flat, preferred_element_type=jnp.float32)
    squares_hi = resid_squares.astype(jnp.bfloat16)
    squares_lo = (resid_squares - squares_hi.astype(jnp.float32)).astype(jnp.bfloat16)
    sent2 = jnp.pad(partial2.astype(jnp.bfloat16), ((0, 0), (0, 2)))
    sent2 = sent2.at[:, 2 * hidden_local].set(squares_hi)
    sent2 = sent2.at[:, 2 * hidden_local + 1].set(squares_lo)
    n_wide = lax.axis_size("wide")
    received2 = lax.all_to_all(
        sent2.reshape(n_wide, sent2.shape[0] // n_wide, sent2.shape[1]), "wide", 0, 0, tiled=False
    )
    summed2 = jnp.sum(received2.astype(jnp.float32), axis=0)
    total_squares2 = summed2[:, 2 * hidden_local] + summed2[:, 2 * hidden_local + 1]
    inv_rms2 = 1.0 / jnp.sqrt(total_squares2 / D + norm_eps)
    gate_up = summed2[:, : 2 * hidden_local] * inv_rms2[:, None]
    hidden = (jax.nn.silu(gate_up[:, :hidden_local]) * gate_up[:, hidden_local:]).astype(
        jnp.bfloat16
    )
    down_partial = jnp.dot(gather_rows(hidden, "wide"), down_weight, preferred_element_type=jnp.float32)
    mlp_out = sum_all(down_partial, "narrow")
    return (resid_float + mlp_out).astype(jnp.bfloat16)


def solution(mesh):
    in_specs = (
        P(None, "wide"),
        P("wide"),
        P("wide", "narrow", None, None),
        P("narrow", None, None),
        P("wide", "narrow", None, None),
        P("wide", "narrow", None, None),
        P("wide", None, None),
        P("wide"),
        P("narrow", "wide"),
        P("wide"),
        P("wide", None, "narrow"),
        P("narrow", "wide"),
    )
    out_specs = P(None, "wide")
    return jax.shard_map(local, mesh=mesh, in_specs=in_specs, out_specs=out_specs, check_vma=False)
```

```python
import math

import jax
import jax.numpy as jnp
from jax import lax
from jax.sharding import PartitionSpec as P

D = 8192
DH = 128
CACHE = 4096


norm_eps = 1e-06
rope_base = 1000000.0


def cos_sin(angle):
    k = jnp.round(angle * 0.6366197723675814)
    r = ((angle - k * 1.5703125) - k * 4.837512969970703125e-4) - k * 7.54978995489188216e-8
    z = r * r
    s = r + r * z * (-1.6666654611e-1 + z * (8.3321608736e-3 + z * -1.9515295891e-4))
    c = 1.0 - 0.5 * z + z * z * (
        4.166664568298827e-2 + z * (-1.388731625493765e-3 + z * 2.443315711809948e-5)
    )
    quadrant = k - 4.0 * jnp.floor(k * 0.25)
    odd = (quadrant == 1.0) | (quadrant == 3.0)
    cos_sign = jnp.where((quadrant == 1.0) | (quadrant == 2.0), -1.0, 1.0)
    sin_sign = jnp.where(quadrant >= 2.0, -1.0, 1.0)
    return cos_sign * jnp.where(odd, s, c), sin_sign * jnp.where(odd, c, s)


def mrope_tables(position):
    half_width = DH // 2
    pair_index = jnp.arange(half_width)
    inv_freq = jnp.exp(pair_index.astype(jnp.float32) * (-2.0 * math.log(rope_base) / DH))
    component = (pair_index >= DH // 8).astype(jnp.int32) + (
        pair_index >= DH // 8 + 3 * DH // 16
    ).astype(jnp.int32)
    pos_float = position.astype(jnp.float32)
    chosen = jnp.where(
        component == 0,
        pos_float[..., 0, :, None],
        jnp.where(component == 1, pos_float[..., 1, :, None], pos_float[..., 2, :, None]),
    )
    angles = chosen * inv_freq
    return cos_sin(angles)


def rotate(values, cosine, sine_table):
    half_width = values.shape[-1] // 2
    leading = values[..., :half_width]
    trailing = values[..., half_width:]
    return jnp.concatenate(
        [leading * cosine - trailing * sine_table, trailing * cosine + leading * sine_table],
        axis=-1,
    )


def reduce_rows(x, axis):
    n = lax.axis_size(axis)
    blocks = x.reshape(n, x.shape[0] // n, x.shape[1])
    return jnp.sum(lax.all_to_all(blocks, axis, 0, 0, tiled=False), axis=0)


def gather_rows(x, axis):
    n = lax.axis_size(axis)
    copies = jnp.broadcast_to(x[None], (n,) + x.shape)
    return lax.all_to_all(copies, axis, 0, 0, tiled=False).reshape(n * x.shape[0], x.shape[1])


def sum_all(x, axis):
    n = lax.axis_size(axis)

    def sent(v):
        return v.astype(jnp.bfloat16)

    def exchange(v, pairs):
        return lax.ppermute(v, axis, pairs).astype(jnp.float32)

    own = sent(x)
    x = own.astype(jnp.float32) + exchange(own, [(i, i ^ 1) for i in range(n)])
    groups = n // 2
    if groups == 4:
        own = sent(x)

        def shifted(k):
            return exchange(own, [(i, ((i // 2 + k) % groups) * 2 + i % 2) for i in range(n)])

        return (own.astype(jnp.float32) + shifted(2)) + (shifted(1) + shifted(3))
    step = 2
    while step < n:
        own = sent(x)
        x = own.astype(jnp.float32) + exchange(own, [(i, i ^ step) for i in range(n)])
        step *= 2
    return x


def local(
    hidden_in,
    attn_gain,
    qkv_weight,
    qkv_bias,
    cache_keys,
    cache_values,
    positions,
    lengths,
    out_weight,
    mlp_gain,
    gate_up_weight,
    down_weight,
):
    score_scale = 1.0 / math.sqrt(DH)
    owned = lengths.shape[0]
    local_rows = hidden_in.shape[1]
    kv_local = qkv_weight.shape[1]
    slot_count = qkv_weight.shape[2]
    group_size = slot_count - 2
    width = kv_local * slot_count * DH
    inputs = hidden_in.astype(jnp.float32)
    local_squares = jnp.sum(inputs * inputs, axis=1)
    scaled = (inputs * attn_gain.astype(jnp.float32)).astype(jnp.bfloat16)
    weight_flat = qkv_weight.reshape(local_rows, width)
    weight_by_slot = qkv_weight.reshape(local_rows, slot_count * kv_local, DH).transpose(1, 0, 2)
    partial = lax.dot_general(
        jnp.broadcast_to(scaled[None], (slot_count * kv_local,) + scaled.shape),
        weight_by_slot,
        (((2,), (1,)), ((0,), (0,))),
        preferred_element_type=jnp.float32,
    )
    partial = partial.transpose(1, 0, 2).reshape(scaled.shape[0], width)
    summed = reduce_rows(jnp.concatenate([partial, local_squares[:, None]], axis=1), "wide")
    inv_rms = 1.0 / jnp.sqrt(summed[:, width] / D + norm_eps)
    projected = inv_rms[:, None] * summed[:, :width] + qkv_bias.reshape(width).astype(jnp.float32)
    projected = projected.reshape(owned, kv_local, slot_count, DH)
    cosine, sine_table = mrope_tables(positions)
    half_width = DH // 2
    keys_lead = cache_keys[..., :half_width].astype(jnp.float32)
    keys_trail = cache_keys[..., half_width:].astype(jnp.float32)
    cos_keys, sin_keys = cosine[:, None], sine_table[:, None]
    keys_rot = jnp.concatenate(
        [keys_lead * cos_keys - keys_trail * sin_keys, keys_trail * cos_keys + keys_lead * sin_keys],
        axis=-1,
    ).astype(jnp.bfloat16)
    at_new_slot = jnp.arange(CACHE)[None, None, :] == lengths[:, None, None]
    new_position = jnp.sum(jnp.where(at_new_slot, positions, 0), axis=2, keepdims=True)
    cos_new, sin_new = mrope_tables(new_position)
    query = rotate(projected[:, :, :group_size], cos_new[:, None], sin_new[:, None]).astype(
        jnp.bfloat16
    )
    key_new = rotate(projected[:, :, group_size], cos_new, sin_new).astype(jnp.bfloat16)
    value_new = projected[:, :, group_size + 1].astype(jnp.bfloat16)
    scores = (
        jnp.einsum("rgjd,rgsd->rgjs", query, keys_rot, preferred_element_type=jnp.float32)
        * score_scale
    )
    own_score = (
        jnp.sum(query.astype(jnp.float32) * key_new.astype(jnp.float32)[:, :, None, :], axis=3)
        * score_scale
    )
    valid_slot = jnp.arange(CACHE)[None, None, None, :] < lengths[:, None, None, None]
    row_max = jnp.maximum(jnp.max(jnp.where(valid_slot, scores, -jnp.inf), axis=3), own_score)
    probabilities = jnp.where(valid_slot, jnp.exp(scores - row_max[..., None]), 0.0)
    own_prob = jnp.exp(own_score - row_max)
    totals = jnp.sum(probabilities, axis=3) + own_prob
    probs_rounded = probabilities.astype(jnp.bfloat16)
    own_rounded = own_prob.astype(jnp.bfloat16).astype(jnp.float32)
    weighted = jnp.einsum(
        "rgjs,rgsd->rgjd", probs_rounded, cache_values, preferred_element_type=jnp.float32
    )
    weighted = weighted + own_rounded[..., None] * value_new.astype(jnp.float32)[:, :, None, :]
    attended = (
        (weighted / totals[..., None])
        .astype(jnp.bfloat16)
        .reshape(owned, kv_local * group_size * DH)
    )
    head_partial = jnp.dot(
        gather_rows(attended, "wide"),
        out_weight,
        preferred_element_type=jnp.float32,
    )
    attn_out = sum_all(head_partial, "narrow")
    residual = (inputs + attn_out).astype(jnp.bfloat16)
    resid_float = residual.astype(jnp.float32)
    resid_squares = jnp.sum(resid_float * resid_float, axis=1)
    scaled2 = (resid_float * mlp_gain.astype(jnp.float32)).astype(jnp.bfloat16)
    hidden_local = gate_up_weight.shape[2]
    gate_up_flat = gate_up_weight.reshape(local_rows, 2 * hidden_local)
    partial2 = jnp.dot(scaled2, gate_up_flat, preferred_element_type=jnp.float32)
    squares_hi = resid_squares.astype(jnp.bfloat16)
    squares_lo = (resid_squares - squares_hi.astype(jnp.float32)).astype(jnp.bfloat16)
    sent2 = jnp.pad(partial2.astype(jnp.bfloat16), ((0, 0), (0, 2)))
    sent2 = sent2.at[:, 2 * hidden_local].set(squares_hi)
    sent2 = sent2.at[:, 2 * hidden_local + 1].set(squares_lo)
    n_wide = lax.axis_size("wide")
    received2 = lax.all_to_all(
        sent2.reshape(n_wide, sent2.shape[0] // n_wide, sent2.shape[1]), "wide", 0, 0, tiled=False
    )
    summed2 = jnp.sum(received2.astype(jnp.float32), axis=0)
    total_squares2 = summed2[:, 2 * hidden_local] + summed2[:, 2 * hidden_local + 1]
    inv_rms2 = 1.0 / jnp.sqrt(total_squares2 / D + norm_eps)
    gate_up = summed2[:, : 2 * hidden_local] * inv_rms2[:, None]
    hidden = (jax.nn.silu(gate_up[:, :hidden_local]) * gate_up[:, hidden_local:]).astype(
        jnp.bfloat16
    )
    down_partial = jnp.dot(gather_rows(hidden, "wide"), down_weight, preferred_element_type=jnp.float32)
    mlp_out = sum_all(down_partial, "narrow")
    return (resid_float + mlp_out).astype(jnp.bfloat16)


def solution(mesh):
    in_specs = (
        P(None, "wide"),
        P("wide"),
        P("wide", "narrow", None, None),
        P("narrow", None, None),
        P("wide", "narrow", None, None),
        P("wide", "narrow", None, None),
        P("wide", None, None),
        P("wide"),
        P("narrow", "wide"),
        P("wide"),
        P("wide", None, "narrow"),
        P("narrow", "wide"),
    )
    out_specs = P(None, "wide")
    return jax.shard_map(local, mesh=mesh, in_specs=in_specs, out_specs=out_specs, check_vma=False)
```
